32 devices in a mesh: users: 16 (over z, y, core), items: 2 (over x).
Axes of the slice: x: 2, y: 2, z: 4, core: 2. Of those that a mesh axis runs over, the one named last changes fastest.
Arguments:
- ratings: bfloat16 [64, 6, 128, 128], P('users', 'items')
- residual: bfloat16 [64, 6, 128, 128], P('users', 'items')
- tile_columns: int32 [64, 6], P('users', 'items'), may hold values from 0 to 2, as said below
- occupied: int32 [64, 6], P('users', 'items'), may hold values from 0 to 1, as said below
- chosen: int32 [64], P('users'), may hold values from 0 to 1, as said below
- user_factors: bfloat16 [64, 8192], P(None, 'users'), may hold values from -5 to 5
- item_factors: bfloat16 [2, 64, 384], P('items'), may hold values from -5 to 5
- start_block: bfloat16 [2, 32, 384], P('items'), may hold values from -0.5 to 0.5
Outputs:
- updated: bfloat16 [64, 6, 128, 128], P('users', 'items')
- left_block: float32 [32, 8192], P(None, 'users')
- right_block: float32 [2, 32, 384], P('items')
The draws below stay inside these ranges and needn't reach their ends.
Inputs may be any that keep to these rules, and one draw needn't show every extreme that they name: `tile_columns`: within one tile row and one item block the 3 slots name different tile columns. Within one tile row and one item block the occupied slots come first, at least one is occupied, and some tile rows have all 3 occupied. Exactly 16 tile rows are chosen.
All inputs are finite; a program needn't handle non-finite values.
Results may differ from the reference program's by a relative error of at most 0.0033.
Values sent between devices are 32-bit elements; how exact they have to be, the bound alone decides.
No kernel may reach another device: no remote copies, remote signals or barrier semaphores. Data moves between devices by JAX's collectives and lax.ppermute only.
A program may use at most 64 MiB of HBM per device.

```python
import math
import jax
import jax.numpy as jnp
from jax import lax

TILE = 128
RANK = 64
BLK = 32
KS = 3
ITILES = 3
NUT = 64
NU = 8192
SLOTS = 6
IB = 384
NI = 768
N_ITEMS = 2


def row_scales(key, widest):
    positions = jnp.arange(NU, dtype=jnp.float32)
    spread = jax.random.uniform(key, (NU,), jnp.float32, 0.0, 1.0)
    scales = 0.3 * jnp.exp(math.log(widest) * spread) * (1.0 + 2.0 * positions / (NU - 1))
    return scales.reshape(NUT, 1, TILE, 1)


def draw_ratings(key, part):
    first, second = jax.random.split(jax.random.fold_in(key, 101))
    values = jax.random.normal(second, (NUT, SLOTS, TILE, TILE), jnp.float32)
    scales = row_scales(first, 10.0)
    return (values * scales).astype(jnp.bfloat16)


def draw_residual(key, part):
    first, second = jax.random.split(jax.random.fold_in(key, 202))
    values = jax.random.normal(second, (NUT, SLOTS, TILE, TILE), jnp.float32)
    scales = row_scales(first, 10.0)
    return (values * scales).astype(jnp.bfloat16)


def draw_tile_columns(key, part):
    several = jax.random.split(jax.random.fold_in(key, 303), NUT * N_ITEMS)
    orders = jax.vmap(lambda single: jax.random.permutation(single, ITILES))(several)
    return orders[:, :KS].reshape(NUT, SLOTS).astype(jnp.int32)


def draw_occupied(key, part):
    counts = jax.random.randint(jax.random.fold_in(key, 404), (NUT, N_ITEMS), 1, KS + 1)
    tile_rows = jnp.arange(NUT, dtype=jnp.int32)[:, None]
    counts = jnp.where(tile_rows % 5 == 0, KS, counts)
    slot_index = jnp.arange(KS, dtype=jnp.int32)[None, None, :]
    return (slot_index < counts[:, :, None]).astype(jnp.int32).reshape(NUT, SLOTS)


def draw_chosen(key, part):
    order = jax.random.permutation(jax.random.fold_in(key, 505), NUT)
    return (order < NUT // 4).astype(jnp.int32)


def shard_levels(key, extent, cuts, least, largest):
    loudness, own = 1.0, jax.random.fold_in(key, 6)
    for position, parts in cuts:
        draws = jnp.exp(jax.random.uniform(jax.random.fold_in(own, position), (parts,), jnp.float32, least / len(cuts), largest / len(cuts)))
        loudness = loudness * jnp.repeat(draws, extent[position] // parts).reshape([-1 if axis == position else 1 for axis in range(len(extent))])
    return loudness


def centred(stream_key, extent, scale, reach, shards=(), kind=jnp.bfloat16):
    values = scale * jax.random.normal(stream_key, extent, jnp.float32)
    if shards:
        values = values * shard_levels(stream_key, extent, shards, -0.22, 0.18)
    return jnp.clip(values, -reach, reach).astype(kind)


def setup_inputs(seed: int = 0) -> dict:
    key_of = jax.random.split(jax.random.key(seed), 9)
    ratings = draw_ratings(jax.random.fold_in(key_of[8], 71), 0)
    residual = draw_residual(jax.random.fold_in(key_of[8], 71), 0)
    tile_columns = draw_tile_columns(jax.random.fold_in(key_of[8], 71), 0)
    occupied = draw_occupied(jax.random.fold_in(key_of[8], 71), 0)
    chosen = draw_chosen(jax.random.fold_in(key_of[8], 71), 0)
    user_factors = centred(key_of[5], (RANK, NU), 0.35, 5.0, ((1, 16),))
    item_factors = centred(key_of[6], (N_ITEMS, RANK, IB), 0.35, 5.0, ((0, 2),))
    start_block = centred(key_of[7], (N_ITEMS, BLK, IB), (NI ** -0.5), 0.5, ((0, 2),))
    return {"ratings": ratings, "residual": residual, "tile_columns": tile_columns, "occupied": occupied, "chosen": chosen, "user_factors": user_factors, "item_factors": item_factors, "start_block": start_block}


def reference(ratings, residual, tile_columns, occupied, chosen, user_factors, item_factors, start_block):
    item_tiles = item_factors.reshape(N_ITEMS, RANK, ITILES, TILE).transpose(0, 2, 1, 3).reshape(N_ITEMS * ITILES, RANK, TILE)
    start_tiles = start_block.reshape(N_ITEMS, BLK, ITILES, TILE).transpose(0, 2, 1, 3).reshape(N_ITEMS * ITILES, BLK, TILE)
    global_tiles = (jnp.arange(SLOTS, dtype=jnp.int32) // KS * ITILES)[None, :] + tile_columns.astype(jnp.int32)
    user_tiles = user_factors.reshape(RANK, NUT, TILE).transpose(1, 0, 2)

    def update_row(inputs):
        rating_row, residual_row, index_row, live_row, chosen_one, user_row = inputs
        factors = item_tiles[index_row].astype(jnp.float32)
        estimate = jnp.einsum('ra,srb->sab', user_row.astype(jnp.float32), factors)
        live_slot = (live_row > 0)[:, None, None]
        selected = live_slot & (chosen_one > 0)
        fresh = jnp.where(selected, rating_row.astype(jnp.float32) - estimate, residual_row.astype(jnp.float32))
        fresh = jnp.where(live_slot, fresh, jnp.float32(0.0)).astype(jnp.bfloat16)
        starts = start_tiles[index_row].astype(jnp.float32)
        product = jnp.einsum('sab,sjb->ja', fresh.astype(jnp.float32), starts)
        return (fresh, product)
    updated, products = lax.map(update_row, (ratings, residual, global_tiles, occupied, chosen, user_tiles))
    projected = products.transpose(1, 0, 2).reshape(BLK, NU)
    gram = jnp.dot(projected, projected.T, precision=lax.Precision.HIGHEST) / NU
    lower = jnp.linalg.cholesky(gram)
    left_block = jax.scipy.linalg.solve_triangular(lower, projected, lower=True)
    left_rounded = left_block.astype(jnp.bfloat16).reshape(BLK, NUT, TILE).transpose(1, 0, 2)

    def accumulate(carry, inputs):
        fresh, index_row, left_row = inputs
        contrib = jnp.einsum('sab,ja->sjb', fresh.astype(jnp.float32), left_row.astype(jnp.float32))
        return (carry.at[index_row].add(contrib), jnp.float32(0.0))
    initial = jnp.zeros((N_ITEMS * ITILES, BLK, TILE), jnp.float32)
    summed, ignored = lax.scan(accumulate, initial, (updated, global_tiles, left_rounded))
    summed = summed.reshape(N_ITEMS, ITILES, BLK, TILE).transpose(0, 2, 1, 3).reshape(N_ITEMS, BLK, IB)
    root = float(NU) ** 0.5
    start_term = jnp.einsum('ji,bjn->bin', lower, start_block.astype(jnp.float32), precision=lax.Precision.HIGHEST)
    right_block = summed / root - root * start_term
    return (updated, left_block, right_block)
```

```python
import jax
import jax.numpy as jnp
from jax import lax
from jax.sharding import PartitionSpec as P


def all_sum(x, axis):
    n = lax.axis_size(axis)
    if n & (n - 1):
        return lax.psum(x, axis)
    step = 1
    while step < n:
        x = x + lax.ppermute(x, axis, [(i, i ^ step) for i in range(n)])
        step *= 2
    return x


def local(
    ratings, residual, tile_columns, occupied, chosen, user_factors, item_factors, start_block
):
    rows_dev = ratings.shape[0]
    width = ratings.shape[2]
    rank_size = user_factors.shape[0]
    block_size = start_block.shape[1]
    item_count = item_factors.shape[2] // width
    user_total = user_factors.shape[1] * lax.axis_size("users")
    root = float(user_total) ** 0.5
    item_tiles = item_factors[0].reshape(rank_size, item_count, width)
    factors = jnp.take(item_tiles, tile_columns, axis=1)
    user_tiles = user_factors.reshape(rank_size, rows_dev, width)
    estimate = jnp.einsum("rta,rtkb->tkab", user_tiles, factors, preferred_element_type=jnp.float32)
    live_slot = (occupied > 0)[:, :, None, None]
    selected = live_slot & (chosen > 0)[:, None, None, None]
    updated = jnp.where(
        selected, ratings.astype(jnp.float32) - estimate, residual.astype(jnp.float32)
    )
    updated = jnp.where(live_slot, updated, jnp.float32(0.0)).astype(jnp.bfloat16)
    start_tiles = jnp.take(
        start_block[0].reshape(block_size, item_count, width), tile_columns, axis=1
    )
    partial_products = jnp.einsum(
        "tkab,jtkb->jta", updated, start_tiles, preferred_element_type=jnp.float32
    )
    projected = all_sum(partial_products.reshape(block_size, rows_dev * width), "items")
    gram_part = jnp.dot(projected, projected.T, precision=lax.Precision.HIGHEST)
    slot_terms = jnp.einsum(
        "jta,tkab->jtkb",
        projected.reshape(block_size, rows_dev, width),
        updated.astype(jnp.float32),
        precision=lax.Precision.HIGHEST,
    )
    one_hot = (
        tile_columns[:, :, None] == jnp.arange(item_count, dtype=jnp.int32)[None, None, :]
    ).astype(jnp.float32)
    item_terms = jnp.einsum("jtkb,tkc->jcb", slot_terms, one_hot, precision=lax.Precision.HIGHEST)
    item_terms = item_terms.reshape(block_size, item_count * width)
    reduced = all_sum(jnp.concatenate([gram_part, item_terms], axis=1), "users")
    gram = reduced[:, :block_size] / user_total
    lower = jnp.linalg.cholesky(gram)
    solved = jax.scipy.linalg.solve_triangular(
        lower, jnp.concatenate([projected, reduced[:, block_size:]], axis=1), lower=True
    )
    left_block = solved[:, : rows_dev * width]
    summed = solved[:, rows_dev * width :].reshape(1, block_size, item_count * width)
    start_term = jnp.einsum(
        "ji,bjn->bin", lower, start_block.astype(jnp.float32), precision=lax.Precision.HIGHEST
    )
    right_block = summed / root - root * start_term
    return (updated, left_block, right_block)


def solution(mesh):
    placed = (
        P("users", "items", None, None),
        P("users", "items", None, None),
        P("users", "items"),
        P("users", "items"),
        P("users"),
        P(None, "users"),
        P("items", None, None),
        P("items", None, None),
    )
    return jax.shard_map(
        local,
        mesh=mesh,
        in_specs=placed,
        out_specs=(P("users", "items", None, None), P(None, "users"), P("items", None, None)),
        check_vma=False,
    )
```

```python
import jax
import jax.numpy as jnp
from jax import lax
from jax.sharding import PartitionSpec as P


def all_sum(x, axis):
    n = lax.axis_size(axis)
    if n & (n - 1):
        return lax.psum(x, axis)
    step = 1
    while step < n:
        x = x + lax.ppermute(x, axis, [(i, i ^ step) for i in range(n)])
        step *= 2
    return x


def local(
    ratings, residual, tile_columns, occupied, chosen, user_factors, item_factors, start_block
):
    rows_dev = ratings.shape[0]
    width = ratings.shape[2]
    rank_size = user_factors.shape[0]
    block_size = start_block.shape[1]
    item_count = item_factors.shape[2] // width
    user_total = user_factors.shape[1] * lax.axis_size("users")
    root = float(user_total) ** 0.5
    item_tiles = item_factors[0].reshape(rank_size, item_count, width)
    factors = jnp.take(item_tiles, tile_columns, axis=1)
    user_tiles = user_factors.reshape(rank_size, rows_dev, width)
    estimate = jnp.einsum("rta,rtkb->tkab", user_tiles, factors, preferred_element_type=jnp.float32)
    live_slot = (occupied > 0)[:, :, None, None]
    selected = live_slot & (chosen > 0)[:, None, None, None]
    updated = jnp.where(
        selected, ratings.astype(jnp.float32) - estimate, residual.astype(jnp.float32)
    )
    updated = jnp.where(live_slot, updated, jnp.float32(0.0)).astype(jnp.bfloat16)
    start_tiles = jnp.take(
        start_block[0].reshape(block_size, item_count, width), tile_columns, axis=1
    )
    partial_products = jnp.einsum(
        "tkab,jtkb->jta", updated, start_tiles, preferred_element_type=jnp.float32
    )
    projected = all_sum(partial_products.reshape(block_size, rows_dev * width), "items")
    gram_part = jnp.dot(projected, projected.T, precision=lax.Precision.HIGHEST)
    slot_terms = jnp.einsum(
        "jta,tkab->jtkb",
        projected.reshape(block_size, rows_dev, width),
        updated.astype(jnp.float32),
        precision=lax.Precision.HIGHEST,
    )
    one_hot = (
        tile_columns[:, :, None] == jnp.arange(item_count, dtype=jnp.int32)[None, None, :]
    ).astype(jnp.float32)
    item_terms = jnp.einsum("jtkb,tkc->jcb", slot_terms, one_hot, precision=lax.Precision.HIGHEST)
    item_terms = item_terms.reshape(block_size, item_count * width)
    payload = jnp.concatenate([gram_part.reshape(-1), item_terms.reshape(-1)])
    reduced = all_sum(payload.reshape(-1, width), "users").reshape(-1)
    gram = reduced[: block_size * block_size].reshape(block_size, block_size) / user_total
    item_sums = reduced[block_size * block_size :].reshape(block_size, item_count * width)
    lower = jnp.linalg.cholesky(gram)
    solved = jax.scipy.linalg.solve_triangular(
        lower, jnp.concatenate([projected, item_sums], axis=1), lower=True
    )
    left_block = solved[:, : rows_dev * width]
    summed = solved[:, rows_dev * width :].reshape(1, block_size, item_count * width)
    start_term = jnp.einsum(
        "ji,bjn->bin", lower, start_block.astype(jnp.float32), precision=lax.Precision.HIGHEST
    )
    right_block = summed / root - root * start_term
    return (updated, left_block, right_block)


def solution(mesh):
    placed = (
        P("users", "items", None, None),
        P("users", "items", None, None),
        P("users", "items"),
        P("users", "items"),
        P("users"),
        P(None, "users"),
        P("items", None, None),
        P("items", None, None),
    )
    return jax.shard_map(
        local,
        mesh=mesh,
        in_specs=placed,
        out_specs=(P("users", "items", None, None), P(None, "users"), P("items", None, None)),
        check_vma=False,
    )
```

```python
import functools

import jax
import jax.numpy as jnp
from jax import lax
from jax.experimental import pallas as pl
from jax.experimental.pallas import tpu as pltpu
from jax.sharding import PartitionSpec as P


def all_sum(x, axis):
    n = lax.axis_size(axis)
    if n & (n - 1):
        return lax.psum(x, axis)
    step = 1
    while step < n:
        x = x + lax.ppermute(x, axis, [(i, i ^ step) for i in range(n)])
        step *= 2
    return x


def tail_kernel(gram_ref, proj_ref, sums_ref, start_ref, left_ref, right_ref, *, scale, root):
    n = gram_ref.shape[0]
    a = gram_ref[...] * scale
    a = 0.5 * (a + a.T)
    rows = lax.broadcasted_iota(jnp.int32, (n, n), 0)
    cols = lax.broadcasted_iota(jnp.int32, (n, n), 1)
    lower = jnp.zeros((n, n), jnp.float32)
    upper = jnp.zeros((n, n), jnp.float32)
    for k in range(n):
        pivot = jnp.sqrt(a[k : k + 1, k : k + 1])
        col = jnp.where(rows[:, k : k + 1] >= k, a[:, k : k + 1] / pivot, 0.0)
        row = jnp.where(cols[k : k + 1, :] >= k, a[k : k + 1, :] / pivot, 0.0)
        a = a - col * row
        lower = jnp.where(cols == k, col, lower)
        upper = jnp.where(rows == k, row, upper)
    inverse = (rows == cols).astype(jnp.float32)
    for k in range(n):
        head = inverse[k : k + 1, :] / lower[k : k + 1, k : k + 1]
        below = jnp.where(rows[:, k : k + 1] > k, lower[:, k : k + 1], 0.0)
        inverse = jnp.where(rows == k, head, inverse - below * head)
    hi = lax.Precision.HIGHEST
    left_ref[...] = jnp.dot(inverse, proj_ref[...], precision=hi, preferred_element_type=jnp.float32)
    summed = jnp.dot(inverse, sums_ref[...], precision=hi, preferred_element_type=jnp.float32)
    start_term = jnp.dot(
        upper, start_ref[...].astype(jnp.float32), precision=hi, preferred_element_type=jnp.float32
    )
    right_ref[...] = summed / root - root * start_term


def tail(gram, projected, item_sums, start, user_total):
    n, users = projected.shape
    items = item_sums.shape[1]
    vmem = pl.BlockSpec(memory_space=pltpu.VMEM)
    return pl.pallas_call(
        functools.partial(tail_kernel, scale=1.0 / user_total, root=float(user_total) ** 0.5),
        out_shape=(
            jax.ShapeDtypeStruct((n, users), jnp.float32),
            jax.ShapeDtypeStruct((n, items), jnp.float32),
        ),
        in_specs=[vmem] * 4,
        out_specs=(vmem, vmem),
        cost_estimate=pl.CostEstimate(
            flops=2 * n * n * (users + 2 * items) * 6, transcendentals=n, bytes_accessed=4 * n * (n + 2 * users + 3 * items)
        ),
    )(gram, projected, item_sums, start)


def local(
    ratings, residual, tile_columns, occupied, chosen, user_factors, item_factors, start_block
):
    rows_dev = ratings.shape[0]
    width = ratings.shape[2]
    rank_size = user_factors.shape[0]
    block_size = start_block.shape[1]
    item_count = item_factors.shape[2] // width
    user_total = user_factors.shape[1] * lax.axis_size("users")
    root = float(user_total) ** 0.5
    item_tiles = item_factors[0].reshape(rank_size, item_count, width)
    factors = jnp.take(item_tiles, tile_columns, axis=1)
    user_tiles = user_factors.reshape(rank_size, rows_dev, width)
    estimate = jnp.einsum("rta,rtkb->tkab", user_tiles, factors, preferred_element_type=jnp.float32)
    live_slot = (occupied > 0)[:, :, None, None]
    selected = live_slot & (chosen > 0)[:, None, None, None]
    updated = jnp.where(
        selected, ratings.astype(jnp.float32) - estimate, residual.astype(jnp.float32)
    )
    updated = jnp.where(live_slot, updated, jnp.float32(0.0)).astype(jnp.bfloat16)
    start_tiles = jnp.take(
        start_block[0].reshape(block_size, item_count, width), tile_columns, axis=1
    )
    partial_products = jnp.einsum(
        "tkab,jtkb->jta", updated, start_tiles, preferred_element_type=jnp.float32
    )
    projected = all_sum(partial_products.reshape(block_size, rows_dev * width), "items")
    gram_part = jnp.dot(projected, projected.T, precision=lax.Precision.HIGHEST)
    slot_terms = jnp.einsum(
        "jta,tkab->jtkb",
        projected.reshape(block_size, rows_dev, width),
        updated.astype(jnp.float32),
        precision=lax.Precision.HIGHEST,
    )
    one_hot = (
        tile_columns[:, :, None] == jnp.arange(item_count, dtype=jnp.int32)[None, None, :]
    ).astype(jnp.float32)
    item_terms = jnp.einsum("jtkb,tkc->jcb", slot_terms, one_hot, precision=lax.Precision.HIGHEST)
    item_terms = item_terms.reshape(block_size, item_count * width)
    payload = jnp.concatenate([gram_part.reshape(-1), item_terms.reshape(-1)])
    reduced = all_sum(payload.reshape(-1, width), "users").reshape(-1)
    gram = reduced[: block_size * block_size].reshape(block_size, block_size)
    item_sums = reduced[block_size * block_size :].reshape(block_size, item_count * width)
    left_block, right_block = tail(gram, projected, item_sums, start_block[0], user_total)
    right_block = right_block.reshape(1, block_size, item_count * width)
    return (updated, left_block, right_block)


def solution(mesh):
    placed = (
        P("users", "items", None, None),
        P("users", "items", None, None),
        P("users", "items"),
        P("users", "items"),
        P("users"),
        P(None, "users"),
        P("items", None, None),
        P("items", None, None),
    )
    return jax.shard_map(
        local,
        mesh=mesh,
        in_specs=placed,
        out_specs=(P("users", "items", None, None), P(None, "users"), P("items", None, None)),
        check_vma=False,
    )
```

```python
import functools

import jax
import jax.numpy as jnp
from jax import lax
from jax.experimental import pallas as pl
from jax.experimental.pallas import tpu as pltpu
from jax.sharding import PartitionSpec as P


def all_sum(x, axis):
    n = lax.axis_size(axis)
    if n & (n - 1):
        return lax.psum(x, axis)
    step = 1
    while step < n:
        x = x + lax.ppermute(x, axis, [(i, i ^ step) for i in range(n)])
        step *= 2
    return x


def tail_kernel(reduced_ref, proj_ref, start_ref, left_ref, right_ref, *, scale, root):
    n = start_ref.shape[0]
    lanes = reduced_ref.shape[1] - start_ref.shape[1]
    g = reduced_ref[:, :n] * scale
    g = 0.5 * (g + g.T)
    rows = lax.broadcasted_iota(jnp.int32, (n, 2 * n), 0)
    cols = lax.broadcasted_iota(jnp.int32, (n, 2 * n), 1)
    aug = jnp.concatenate([g, (rows[:, :n] == cols[:, :n]).astype(jnp.float32)], axis=1)
    for k in range(n):
        inv_pivot = lax.rsqrt(aug[k : k + 1, k : k + 1])
        head = aug[k : k + 1, :] * inv_pivot
        factor = jnp.where(rows[:, :1] > k, aug[:, k : k + 1] * inv_pivot, 0.0)
        aug = jnp.where(rows == k, head, aug - factor * head)
    upper = aug[:, :n]
    inverse = aug[:, n:]
    hi = lax.Precision.HIGHEST
    left_ref[...] = jnp.dot(inverse, proj_ref[...], precision=hi, preferred_element_type=jnp.float32)
    summed = jnp.dot(inverse, reduced_ref[:, lanes:], precision=hi, preferred_element_type=jnp.float32)
    start_term = jnp.dot(
        upper, start_ref[...].astype(jnp.float32), precision=hi, preferred_element_type=jnp.float32
    )
    right_ref[...] = summed / root - root * start_term


def tail(reduced, projected, start, user_total):
    n, users = projected.shape
    items = start.shape[1]
    vmem = pl.BlockSpec(memory_space=pltpu.VMEM)
    return pl.pallas_call(
        functools.partial(tail_kernel, scale=1.0 / user_total, root=float(user_total) ** 0.5),
        out_shape=(
            jax.ShapeDtypeStruct((n, users), jnp.float32),
            jax.ShapeDtypeStruct((n, items), jnp.float32),
        ),
        in_specs=[vmem] * 3,
        out_specs=(vmem, vmem),
        cost_estimate=pl.CostEstimate(
            flops=2 * n * n * (users + 2 * items) * 6, transcendentals=n, bytes_accessed=4 * n * (2 * users + 3 * items)
        ),
    )(reduced, projected, start)


def local(
    ratings, residual, tile_columns, occupied, chosen, user_factors, item_factors, start_block
):
    rows_dev = ratings.shape[0]
    width = ratings.shape[2]
    rank_size = user_factors.shape[0]
    block_size = start_block.shape[1]
    item_count = item_factors.shape[2] // width
    user_total = user_factors.shape[1] * lax.axis_size("users")
    root = float(user_total) ** 0.5
    item_tiles = item_factors[0].reshape(rank_size, item_count, width)
    factors = jnp.take(item_tiles, tile_columns, axis=1)
    user_tiles = user_factors.reshape(rank_size, rows_dev, width)
    estimate = jnp.einsum("rta,rtkb->tkab", user_tiles, factors, preferred_element_type=jnp.float32)
    live_slot = (occupied > 0)[:, :, None, None]
    selected = live_slot & (chosen > 0)[:, None, None, None]
    updated = jnp.where(
        selected, ratings.astype(jnp.float32) - estimate, residual.astype(jnp.float32)
    )
    updated = jnp.where(live_slot, updated, jnp.float32(0.0)).astype(jnp.bfloat16)
    start_tiles = jnp.take(
        start_block[0].reshape(block_size, item_count, width), tile_columns, axis=1
    )
    partial_products = jnp.einsum(
        "tkab,jtkb->jta", updated, start_tiles, preferred_element_type=jnp.float32
    )
    projected = all_sum(partial_products.reshape(block_size, rows_dev * width), "items")
    gram_part = jnp.dot(projected, projected.T, precision=lax.Precision.HIGHEST)
    slot_terms = jnp.einsum(
        "jta,tkab->jtkb",
        projected.reshape(block_size, rows_dev, width),
        updated.astype(jnp.float32),
        precision=lax.Precision.HIGHEST,
    )
    one_hot = (
        tile_columns[:, :, None] == jnp.arange(item_count, dtype=jnp.int32)[None, None, :]
    ).astype(jnp.float32)
    item_terms = jnp.einsum("jtkb,tkc->jcb", slot_terms, one_hot, precision=lax.Precision.HIGHEST)
    item_terms = item_terms.reshape(block_size, item_count * width)
    lanes = -(-block_size // width) * width
    gram_lanes = jnp.pad(gram_part, ((0, 0), (0, lanes - block_size)))
    reduced = all_sum(jnp.concatenate([gram_lanes, item_terms], axis=1), "users")
    left_block, right_block = tail(reduced, projected, start_block[0], user_total)
    right_block = right_block.reshape(1, block_size, item_count * width)
    return (updated, left_block, right_block)


def solution(mesh):
    placed = (
        P("users", "items", None, None),
        P("users", "items", None, None),
        P("users", "items"),
        P("users", "items"),
        P("users"),
        P(None, "users"),
        P("items", None, None),
        P("items", None, None),
    )
    return jax.shard_map(
        local,
        mesh=mesh,
        in_specs=placed,
        out_specs=(P("users", "items", None, None), P(None, "users"), P("items", None, None)),
        check_vma=False,
    )
```

```python
import functools

import jax
import jax.numpy as jnp
from jax import lax
from jax.experimental import pallas as pl
from jax.experimental.pallas import tpu as pltpu
from jax.sharding import PartitionSpec as P


def all_sum(x, axis):
    n = lax.axis_size(axis)
    if n & (n - 1):
        return lax.psum(x, axis)
    step = 1
    while step < n:
        x = x + lax.ppermute(x, axis, [(i, i ^ step) for i in range(n)])
        step *= 2
    return x


def tail_kernel(reduced_ref, proj_ref, start_ref, left_ref, right_ref, *, scale, root):
    n = start_ref.shape[0]
    lanes = reduced_ref.shape[1] - start_ref.shape[1]
    g = reduced_ref[:, :n] * scale
    g = 0.5 * (g + g.T)
    rows = lax.broadcasted_iota(jnp.int32, (n, 2 * n), 0)
    cols = lax.broadcasted_iota(jnp.int32, (n, 2 * n), 1)
    aug = jnp.concatenate([g, (rows[:, :n] == cols[:, :n]).astype(jnp.float32)], axis=1)
    for k in range(n):
        inv_pivot = lax.rsqrt(aug[k : k + 1, k : k + 1])
        head = aug[k : k + 1, :] * inv_pivot
        factor = jnp.where(rows[:, :1] > k, aug[:, k : k + 1] * inv_pivot, 0.0)
        aug = jnp.where(rows == k, head, aug - factor * head)
    upper = aug[:, :n]
    inverse = aug[:, n:]
    hi = lax.Precision.HIGHEST
    left_ref[...] = jnp.dot(inverse, proj_ref[...], precision=hi, preferred_element_type=jnp.float32)
    summed = jnp.dot(inverse, reduced_ref[:, lanes:], precision=hi, preferred_element_type=jnp.float32)
    start_term = jnp.dot(
        upper, start_ref[...].astype(jnp.float32), precision=hi, preferred_element_type=jnp.float32
    )
    right_ref[...] = summed / root - root * start_term


def tail(reduced, projected, start, user_total):
    n, users = projected.shape
    items = start.shape[1]
    vmem = pl.BlockSpec(memory_space=pltpu.VMEM)
    return pl.pallas_call(
        functools.partial(tail_kernel, scale=1.0 / user_total, root=float(user_total) ** 0.5),
        out_shape=(
            jax.ShapeDtypeStruct((n, users), jnp.float32),
            jax.ShapeDtypeStruct((n, items), jnp.float32),
        ),
        in_specs=[vmem] * 3,
        out_specs=(vmem, vmem),
        cost_estimate=pl.CostEstimate(
            flops=2 * n * n * (users + 2 * items) * 6, transcendentals=n, bytes_accessed=4 * n * (2 * users + 3 * items)
        ),
    )(reduced, projected, start)


def update_kernel(cols_ref, live_ref, chosen_ref, rat_ref, res_ref, user_ref, item_ref, start_ref, upd_ref, part_ref):
    t = pl.program_id(0)
    width = rat_ref.shape[2]
    slots = rat_ref.shape[1]
    tiles = item_ref.shape[1] // width
    user = user_ref[...]
    pick = chosen_ref[t] > 0
    acc = jnp.zeros(part_ref.shape, jnp.float32)
    for k in range(slots):
        c = cols_ref[t, k]
        live = live_ref[t, k] > 0
        factor = item_ref[:, 0:width]
        start = start_ref[:, 0:width]
        for j in range(1, tiles):
            factor = jnp.where(c == j, item_ref[:, j * width : (j + 1) * width], factor)
            start = jnp.where(c == j, start_ref[:, j * width : (j + 1) * width], start)
        estimate = lax.dot_general(
            user, factor, (((0,), (0,)), ((), ())), preferred_element_type=jnp.float32
        )
        fresh = jnp.where(
            live & pick, rat_ref[0, k].astype(jnp.float32) - estimate, res_ref[0, k].astype(jnp.float32)
        )
        fresh = jnp.where(live, fresh, 0.0).astype(jnp.bfloat16)
        upd_ref[0, k] = fresh
        acc = acc + lax.dot_general(
            start, fresh, (((1,), (1,)), ((), ())), preferred_element_type=jnp.float32
        )
    part_ref[...] = acc


def update(ratings, residual, tile_columns, occupied, chosen, user_factors, items, start):
    rows, slots, width, _ = ratings.shape
    rank = user_factors.shape[0]
    block = start.shape[0]
    smem = pl.BlockSpec(memory_space=pltpu.SMEM)
    tile = pl.BlockSpec((1, slots, width, width), lambda t: (t, 0, 0, 0))
    return pl.pallas_call(
        update_kernel,
        grid=(rows,),
        out_shape=(
            jax.ShapeDtypeStruct(ratings.shape, jnp.bfloat16),
            jax.ShapeDtypeStruct((block, rows * width), jnp.float32),
        ),
        in_specs=[
            smem,
            smem,
            smem,
            tile,
            tile,
            pl.BlockSpec((rank, width), lambda t: (0, t)),
            pl.BlockSpec(items.shape, lambda t: (0, 0)),
            pl.BlockSpec(start.shape, lambda t: (0, 0)),
        ],
        out_specs=(tile, pl.BlockSpec((block, width), lambda t: (0, t))),
        cost_estimate=pl.CostEstimate(
            flops=2 * rows * slots * width * width * (rank + block),
            transcendentals=0,
            bytes_accessed=6 * ratings.size + 4 * block * rows * width,
        ),
    )(tile_columns, occupied, chosen, ratings, residual, user_factors, items, start)


def local(
    ratings, residual, tile_columns, occupied, chosen, user_factors, item_factors, start_block
):
    rows_dev = ratings.shape[0]
    width = ratings.shape[2]
    block_size = start_block.shape[1]
    item_count = item_factors.shape[2] // width
    user_total = user_factors.shape[1] * lax.axis_size("users")
    updated, partial_products = update(
        ratings, residual, tile_columns, occupied, chosen, user_factors, item_factors[0], start_block[0]
    )
    projected = all_sum(partial_products, "items")
    gram_part = jnp.dot(projected, projected.T, precision=lax.Precision.HIGHEST)
    slot_terms = jnp.einsum(
        "jta,tkab->jtkb",
        projected.reshape(block_size, rows_dev, width),
        updated.astype(jnp.float32),
        precision=lax.Precision.HIGHEST,
    )
    one_hot = (
        tile_columns[:, :, None] == jnp.arange(item_count, dtype=jnp.int32)[None, None, :]
    ).astype(jnp.float32)
    item_terms = jnp.einsum("jtkb,tkc->jcb", slot_terms, one_hot, precision=lax.Precision.HIGHEST)
    item_terms = item_terms.reshape(block_size, item_count * width)
    lanes = -(-block_size // width) * width
    gram_lanes = jnp.pad(gram_part, ((0, 0), (0, lanes - block_size)))
    reduced = all_sum(jnp.concatenate([gram_lanes, item_terms], axis=1), "users")
    left_block, right_block = tail(reduced, projected, start_block[0], user_total)
    right_block = right_block.reshape(1, block_size, item_count * width)
    return (updated, left_block, right_block)


def solution(mesh):
    placed = (
        P("users", "items", None, None),
        P("users", "items", None, None),
        P("users", "items"),
        P("users", "items"),
        P("users"),
        P(None, "users"),
        P("items", None, None),
        P("items", None, None),
    )
    return jax.shard_map(
        local,
        mesh=mesh,
        in_specs=placed,
        out_specs=(P("users", "items", None, None), P(None, "users"), P("items", None, None)),
        check_vma=False,
    )
```

```python
import functools

import jax
import jax.numpy as jnp
from jax import lax
from jax.experimental import pallas as pl
from jax.experimental.pallas import tpu as pltpu
from jax.sharding import PartitionSpec as P


def all_sum_parts(x, axis):
    n = lax.axis_size(axis)
    if n & (n - 1):
        return lax.psum(x, axis), jnp.zeros_like(x)
    step = 1
    other = jnp.zeros_like(x)
    while step < n:
        if step > 1:
            x = x + other
        other = lax.ppermute(x, axis, [(i, i ^ step) for i in range(n)])
        step *= 2
    return x, other


def tail_kernel(mine_ref, other_ref, proj_ref, start_ref, left_ref, right_ref, *, scale, root):
    n = start_ref.shape[0]
    lanes = mine_ref.shape[1] - start_ref.shape[1]
    reduced = mine_ref[...] + other_ref[...]
    g = reduced[:, :n] * scale
    g = 0.5 * (g + g.T)
    rows = lax.broadcasted_iota(jnp.int32, (n, 2 * n), 0)
    cols = lax.broadcasted_iota(jnp.int32, (n, 2 * n), 1)
    aug = jnp.concatenate([g, (rows[:, :n] == cols[:, :n]).astype(jnp.float32)], axis=1)
    for k in range(n):
        inv_pivot = lax.rsqrt(aug[k : k + 1, k : k + 1])
        head = aug[k : k + 1, :] * inv_pivot
        factor = jnp.where(rows[:, :1] > k, aug[:, k : k + 1] * inv_pivot, 0.0)
        aug = jnp.where(rows == k, head, aug - factor * head)
    upper = aug[:, :n]
    inverse = aug[:, n:]
    hi = lax.Precision.HIGHEST
    left_ref[...] = jnp.dot(inverse, proj_ref[...], precision=hi, preferred_element_type=jnp.float32)
    summed = jnp.dot(inverse, reduced[:, lanes:], precision=hi, preferred_element_type=jnp.float32)
    start_term = jnp.dot(
        upper, start_ref[...].astype(jnp.float32), precision=hi, preferred_element_type=jnp.float32
    )
    right_ref[...] = summed / root - root * start_term


def tail(mine, other, projected, start, user_total):
    n, users = projected.shape
    items = start.shape[1]
    vmem = pl.BlockSpec(memory_space=pltpu.VMEM)
    return pl.pallas_call(
        functools.partial(tail_kernel, scale=1.0 / user_total, root=float(user_total) ** 0.5),
        out_shape=(
            jax.ShapeDtypeStruct((n, users), jnp.float32),
            jax.ShapeDtypeStruct((n, items), jnp.float32),
        ),
        in_specs=[vmem] * 4,
        out_specs=(vmem, vmem),
        cost_estimate=pl.CostEstimate(
            flops=2 * n * n * (users + 2 * items) * 6, transcendentals=n, bytes_accessed=4 * n * (2 * users + 3 * items)
        ),
    )(mine, other, projected, start)


def mid_kernel(cols_ref, mine_ref, other_ref, upd_ref, proj_ref, pay_ref):
    rows, slots, width, _ = upd_ref.shape
    n = proj_ref.shape[0]
    hi = lax.Precision.HIGHEST
    proj = mine_ref[...] + other_ref[...]
    proj_ref[...] = proj
    gram = lax.dot_general(proj, proj, (((1,), (1,)), ((), ())), precision=hi, preferred_element_type=jnp.float32)
    lanes = pay_ref.shape[1] - tiles_of(pay_ref.shape[1], n, width) * width
    pay_ref[:, 0:lanes] = jnp.pad(gram, ((0, 0), (0, lanes - n)))
    count = tiles_of(pay_ref.shape[1], n, width)
    sums = [jnp.zeros((n, width), jnp.float32) for _ in range(count)]
    for t in range(rows):
        block = proj[:, t * width : (t + 1) * width]
        for k in range(slots):
            c = cols_ref[t, k]
            term = jnp.dot(block, upd_ref[t, k].astype(jnp.float32), precision=hi, preferred_element_type=jnp.float32)
            sums = [sums[j] + jnp.where(c == j, term, 0.0) for j in range(count)]
    for j in range(count):
        pay_ref[:, lanes + j * width : lanes + (j + 1) * width] = sums[j]


def tiles_of(total, n, width):
    return (total - (-(-n // width) * width)) // width


def mid(tile_columns, mine, other, updated, tiles):
    n, users = mine.shape
    width = updated.shape[2]
    lanes = -(-n // width) * width
    vmem = pl.BlockSpec(memory_space=pltpu.VMEM)
    return pl.pallas_call(
        mid_kernel,
        out_shape=(
            jax.ShapeDtypeStruct((n, users), jnp.float32),
            jax.ShapeDtypeStruct((n, lanes + tiles * width), jnp.float32),
        ),
        in_specs=[pl.BlockSpec(memory_space=pltpu.SMEM), vmem, vmem, vmem],
        out_specs=(vmem, vmem),
        cost_estimate=pl.CostEstimate(
            flops=2 * n * users * (n + width) * 6, transcendentals=0, bytes_accessed=2 * updated.size + 16 * n * users
        ),
    )(tile_columns, mine, other, updated)


def update_kernel(cols_ref, live_ref, chosen_ref, rat_ref, res_ref, user_ref, item_ref, start_ref, upd_ref, part_ref):
    t = pl.program_id(0)
    width = rat_ref.shape[2]
    slots = rat_ref.shape[1]
    tiles = item_ref.shape[1] // width
    user = user_ref[...]
    pick = chosen_ref[t] > 0
    factors, starts, lives = [], [], []
    for k in range(slots):
        c = cols_ref[t, k]
        lives.append(live_ref[t, k] > 0)
        factor = item_ref[:, 0:width]
        start = start_ref[:, 0:width]
        for j in range(1, tiles):
            factor = jnp.where(c == j, item_ref[:, j * width : (j + 1) * width], factor)
            start = jnp.where(c == j, start_ref[:, j * width : (j + 1) * width], start)
        factors.append(factor)
        starts.append(start)
    estimate = lax.dot_general(
        user, jnp.concatenate(factors, axis=1), (((0,), (0,)), ((), ())), preferred_element_type=jnp.float32
    )
    fresh = []
    for k in range(slots):
        live = lives[k]
        value = jnp.where(
            live & pick,
            rat_ref[0, k].astype(jnp.float32) - estimate[:, k * width : (k + 1) * width],
            res_ref[0, k].astype(jnp.float32),
        )
        value = jnp.where(live, value, 0.0).astype(jnp.bfloat16)
        upd_ref[0, k] = value
        fresh.append(value)
    acc = lax.dot_general(
        jnp.concatenate(starts, axis=1),
        jnp.concatenate(fresh, axis=1),
        (((1,), (1,)), ((), ())),
        preferred_element_type=jnp.float32,
    )
    part_ref[...] = acc


def update(ratings, residual, tile_columns, occupied, chosen, user_factors, items, start):
    rows, slots, width, _ = ratings.shape
    rank = user_factors.shape[0]
    block = start.shape[0]
    smem = pl.BlockSpec(memory_space=pltpu.SMEM)
    tile = pl.BlockSpec((1, slots, width, width), lambda t: (t, 0, 0, 0))
    return pl.pallas_call(
        update_kernel,
        grid=(rows,),
        out_shape=(
            jax.ShapeDtypeStruct(ratings.shape, jnp.bfloat16),
            jax.ShapeDtypeStruct((block, rows * width), jnp.float32),
        ),
        in_specs=[
            smem,
            smem,
            smem,
            tile,
            tile,
            pl.BlockSpec((rank, width), lambda t: (0, t)),
            pl.BlockSpec(items.shape, lambda t: (0, 0)),
            pl.BlockSpec(start.shape, lambda t: (0, 0)),
        ],
        out_specs=(tile, pl.BlockSpec((block, width), lambda t: (0, t))),
        cost_estimate=pl.CostEstimate(
            flops=2 * rows * slots * width * width * (rank + block),
            transcendentals=0,
            bytes_accessed=6 * ratings.size + 4 * block * rows * width,
        ),
    )(tile_columns, occupied, chosen, ratings, residual, user_factors, items, start)


def local(
    ratings, residual, tile_columns, occupied, chosen, user_factors, item_factors, start_block
):
    rows_dev = ratings.shape[0]
    width = ratings.shape[2]
    block_size = start_block.shape[1]
    item_count = item_factors.shape[2] // width
    user_total = user_factors.shape[1] * lax.axis_size("users")
    updated, partial_products = update(
        ratings, residual, tile_columns, occupied, chosen, user_factors, item_factors[0], start_block[0]
    )
    mine, other = all_sum_parts(partial_products, "items")
    projected, payload = mid(tile_columns, mine, other, updated, item_count)
    mine, other = all_sum_parts(payload, "users")
    left_block, right_block = tail(mine, other, projected, start_block[0], user_total)
    right_block = right_block.reshape(1, block_size, item_count * width)
    return (updated, left_block, right_block)


def solution(mesh):
    placed = (
        P("users", "items", None, None),
        P("users", "items", None, None),
        P("users", "items"),
        P("users", "items"),
        P("users"),
        P(None, "users"),
        P("items", None, None),
        P("items", None, None),
    )
    return jax.shard_map(
        local,
        mesh=mesh,
        in_specs=placed,
        out_specs=(P("users", "items", None, None), P(None, "users"), P("items", None, None)),
        check_vma=False,
    )
```

```python
import functools

import jax
import jax.numpy as jnp
from jax import lax
from jax.experimental import pallas as pl
from jax.experimental.pallas import tpu as pltpu
from jax.sharding import PartitionSpec as P


def all_sum_parts(x, axis):
    n = lax.axis_size(axis)
    if n & (n - 1):
        return lax.psum(x, axis), jnp.zeros_like(x)
    step = 1
    other = jnp.zeros_like(x)
    while step < n:
        if step > 1:
            x = x + other
        other = lax.ppermute(x, axis, [(i, i ^ step) for i in range(n)])
        step *= 2
    return x, other


def tail_kernel(mine_ref, other_ref, proj_ref, start_ref, left_ref, right_ref, *, scale, root):
    n = start_ref.shape[0]
    lanes = mine_ref.shape[1] - start_ref.shape[1]
    reduced = mine_ref[...] + other_ref[...]
    g = reduced[:, :n] * scale
    g = 0.5 * (g + g.T)
    rows = lax.broadcasted_iota(jnp.int32, (n, 2 * n), 0)
    cols = lax.broadcasted_iota(jnp.int32, (n, 2 * n), 1)
    aug = jnp.concatenate([g, (rows[:, :n] == cols[:, :n]).astype(jnp.float32)], axis=1)
    for k in range(n):
        inv_pivot = lax.rsqrt(aug[k : k + 1, k : k + 1])
        head = aug[k : k + 1, :] * inv_pivot
        factor = jnp.where(rows[:, :1] > k, aug[:, k : k + 1] * inv_pivot, 0.0)
        aug = jnp.where(rows == k, head, aug - factor * head)
    upper = aug[:, :n]
    inverse = aug[:, n:]
    hi = lax.Precision.HIGHEST
    left_ref[...] = jnp.dot(inverse, proj_ref[...], precision=hi, preferred_element_type=jnp.float32)
    summed = jnp.dot(inverse, reduced[:, lanes:], precision=hi, preferred_element_type=jnp.float32)
    start_term = jnp.dot(
        upper, start_ref[...].astype(jnp.float32), precision=hi, preferred_element_type=jnp.float32
    )
    right_ref[...] = summed / root - root * start_term


def tail(mine, other, projected, start, user_total):
    n, users = projected.shape
    items = start.shape[1]
    vmem = pl.BlockSpec(memory_space=pltpu.VMEM)
    return pl.pallas_call(
        functools.partial(tail_kernel, scale=1.0 / user_total, root=float(user_total) ** 0.5),
        out_shape=(
            jax.ShapeDtypeStruct((n, users), jnp.float32),
            jax.ShapeDtypeStruct((n, items), jnp.float32),
        ),
        in_specs=[vmem] * 4,
        out_specs=(vmem, vmem),
        cost_estimate=pl.CostEstimate(
            flops=2 * n * n * (users + 2 * items) * 6, transcendentals=n, bytes_accessed=4 * n * (2 * users + 3 * items)
        ),
    )(mine, other, projected, start)


def mid_kernel(cols_ref, mine_ref, other_ref, upd_ref, proj_ref, pay_ref):
    rows, slots, width, _ = upd_ref.shape
    n = proj_ref.shape[0]
    proj = mine_ref[...] + other_ref[...]
    proj_ref[...] = proj
    head = proj.astype(jnp.bfloat16)
    tail = (proj - head.astype(jnp.float32)).astype(jnp.bfloat16)
    nt = (((1,), (1,)), ((), ()))
    f32 = jnp.float32
    gram = lax.dot_general(head, head, nt, preferred_element_type=f32) + (
        lax.dot_general(head, tail, nt, preferred_element_type=f32)
        + lax.dot_general(tail, head, nt, preferred_element_type=f32)
    )
    count = tiles_of(pay_ref.shape[1], n, width)
    lanes = pay_ref.shape[1] - count * width
    pay_ref[:, 0:lanes] = jnp.pad(gram, ((0, 0), (0, lanes - n)))
    sums = [jnp.zeros((n, width), f32) for _ in range(count)]
    for t in range(rows):
        tiles = jnp.concatenate([upd_ref[t, k] for k in range(slots)], axis=1)
        part = slice(t * width, (t + 1) * width)
        term = jnp.dot(head[:, part], tiles, preferred_element_type=f32) + jnp.dot(
            tail[:, part], tiles, preferred_element_type=f32
        )
        for k in range(slots):
            c = cols_ref[t, k]
            piece = term[:, k * width : (k + 1) * width]
            sums = [sums[j] + jnp.where(c == j, piece, 0.0) for j in range(count)]
    for j in range(count):
        pay_ref[:, lanes + j * width : lanes + (j + 1) * width] = sums[j]


def tiles_of(total, n, width):
    return (total - (-(-n // width) * width)) // width


def mid(tile_columns, mine, other, updated, tiles):
    n, users = mine.shape
    width = updated.shape[2]
    lanes = -(-n // width) * width
    vmem = pl.BlockSpec(memory_space=pltpu.VMEM)
    return pl.pallas_call(
        mid_kernel,
        out_shape=(
            jax.ShapeDtypeStruct((n, users), jnp.float32),
            jax.ShapeDtypeStruct((n, lanes + tiles * width), jnp.float32),
        ),
        in_specs=[pl.BlockSpec(memory_space=pltpu.SMEM), vmem, vmem, vmem],
        out_specs=(vmem, vmem),
        cost_estimate=pl.CostEstimate(
            flops=2 * n * users * (n + width) * 3, transcendentals=0, bytes_accessed=2 * updated.size + 16 * n * users
        ),
    )(tile_columns, mine, other, updated)


def update_kernel(cols_ref, live_ref, chosen_ref, rat_ref, res_ref, user_ref, item_ref, start_ref, upd_ref, part_ref):
    t = pl.program_id(0)
    width = rat_ref.shape[2]
    slots = rat_ref.shape[1]
    tiles = item_ref.shape[1] // width
    user = user_ref[...]
    pick = chosen_ref[t] > 0
    factors, starts, lives = [], [], []
    for k in range(slots):
        c = cols_ref[t, k]
        lives.append(live_ref[t, k] > 0)
        factor = item_ref[:, 0:width]
        start = start_ref[:, 0:width]
        for j in range(1, tiles):
            factor = jnp.where(c == j, item_ref[:, j * width : (j + 1) * width], factor)
            start = jnp.where(c == j, start_ref[:, j * width : (j + 1) * width], start)
        factors.append(factor)
        starts.append(start)
    estimate = lax.dot_general(
        user, jnp.concatenate(factors, axis=1), (((0,), (0,)), ((), ())), preferred_element_type=jnp.float32
    )
    fresh = []
    for k in range(slots):
        live = lives[k]
        value = jnp.where(
            live & pick,
            rat_ref[0, k].astype(jnp.float32) - estimate[:, k * width : (k + 1) * width],
            res_ref[0, k].astype(jnp.float32),
        )
        value = jnp.where(live, value, 0.0).astype(jnp.bfloat16)
        upd_ref[0, k] = value
        fresh.append(value)
    acc = lax.dot_general(
        jnp.concatenate(starts, axis=1),
        jnp.concatenate(fresh, axis=1),
        (((1,), (1,)), ((), ())),
        preferred_element_type=jnp.float32,
    )
    part_ref[...] = acc


def update(ratings, residual, tile_columns, occupied, chosen, user_factors, items, start):
    rows, slots, width, _ = ratings.shape
    rank = user_factors.shape[0]
    block = start.shape[0]
    smem = pl.BlockSpec(memory_space=pltpu.SMEM)
    tile = pl.BlockSpec((1, slots, width, width), lambda t: (t, 0, 0, 0))
    return pl.pallas_call(
        update_kernel,
        grid=(rows,),
        out_shape=(
            jax.ShapeDtypeStruct(ratings.shape, jnp.bfloat16),
            jax.ShapeDtypeStruct((block, rows * width), jnp.float32),
        ),
        in_specs=[
            smem,
            smem,
            smem,
            tile,
            tile,
            pl.BlockSpec((rank, width), lambda t: (0, t)),
            pl.BlockSpec(items.shape, lambda t: (0, 0)),
            pl.BlockSpec(start.shape, lambda t: (0, 0)),
        ],
        out_specs=(tile, pl.BlockSpec((block, width), lambda t: (0, t))),
        cost_estimate=pl.CostEstimate(
            flops=2 * rows * slots * width * width * (rank + block),
            transcendentals=0,
            bytes_accessed=6 * ratings.size + 4 * block * rows * width,
        ),
    )(tile_columns, occupied, chosen, ratings, residual, user_factors, items, start)


def local(
    ratings, residual, tile_columns, occupied, chosen, user_factors, item_factors, start_block
):
    rows_dev = ratings.shape[0]
    width = ratings.shape[2]
    block_size = start_block.shape[1]
    item_count = item_factors.shape[2] // width
    user_total = user_factors.shape[1] * lax.axis_size("users")
    updated, partial_products = update(
        ratings, residual, tile_columns, occupied, chosen, user_factors, item_factors[0], start_block[0]
    )
    mine, other = all_sum_parts(partial_products, "items")
    projected, payload = mid(tile_columns, mine, other, updated, item_count)
    mine, other = all_sum_parts(payload, "users")
    left_block, right_block = tail(mine, other, projected, start_block[0], user_total)
    right_block = right_block.reshape(1, block_size, item_count * width)
    return (updated, left_block, right_block)


def solution(mesh):
    placed = (
        P("users", "items", None, None),
        P("users", "items", None, None),
        P("users", "items"),
        P("users", "items"),
        P("users"),
        P(None, "users"),
        P("items", None, None),
        P("items", None, None),
    )
    return jax.shard_map(
        local,
        mesh=mesh,
        in_specs=placed,
        out_specs=(P("users", "items", None, None), P(None, "users"), P("items", None, None)),
        check_vma=False,
    )
```

```python
import functools

import jax
import jax.numpy as jnp
from jax import lax
from jax.experimental import pallas as pl
from jax.experimental.pallas import tpu as pltpu
from jax.sharding import PartitionSpec as P


def all_sum(x, axis):
    n = lax.axis_size(axis)
    if n & (n - 1):
        return lax.psum(x, axis)
    step = 1
    while step < n:
        x = x + lax.ppermute(x, axis, [(i, i ^ step) for i in range(n)])
        step *= 2
    return x


def tail_kernel(reduced_ref, proj_ref, start_ref, left_ref, right_ref, *, scale, root):
    n = start_ref.shape[0]
    lanes = reduced_ref.shape[1] - start_ref.shape[1]
    g = reduced_ref[:, :n] * scale
    g = 0.5 * (g + g.T)
    rows = lax.broadcasted_iota(jnp.int32, (n, 2 * n), 0)
    cols = lax.broadcasted_iota(jnp.int32, (n, 2 * n), 1)
    aug = jnp.concatenate([g, (rows[:, :n] == cols[:, :n]).astype(jnp.float32)], axis=1)
    for k in range(n):
        inv_pivot = lax.rsqrt(aug[k : k + 1, k : k + 1])
        head = aug[k : k + 1, :] * inv_pivot
        factor = jnp.where(rows[:, :1] > k, aug[:, k : k + 1] * inv_pivot, 0.0)
        aug = jnp.where(rows == k, head, aug - factor * head)
    upper = aug[:, :n]
    inverse = aug[:, n:]
    hi = lax.Precision.HIGHEST
    left_ref[...] = jnp.dot(inverse, proj_ref[...], precision=hi, preferred_element_type=jnp.float32)
    summed = jnp.dot(inverse, reduced_ref[:, lanes:], precision=hi, preferred_element_type=jnp.float32)
    start_term = jnp.dot(
        upper, start_ref[...].astype(jnp.float32), precision=hi, preferred_element_type=jnp.float32
    )
    right_ref[...] = summed / root - root * start_term


def tail(reduced, projected, start, user_total):
    n, users = projected.shape
    items = start.shape[1]
    vmem = pl.BlockSpec(memory_space=pltpu.VMEM)
    return pl.pallas_call(
        functools.partial(tail_kernel, scale=1.0 / user_total, root=float(user_total) ** 0.5),
        out_shape=(
            jax.ShapeDtypeStruct((n, users), jnp.float32),
            jax.ShapeDtypeStruct((n, items), jnp.float32),
        ),
        in_specs=[vmem] * 3,
        out_specs=(vmem, vmem),
        cost_estimate=pl.CostEstimate(
            flops=2 * n * n * (users + 2 * items) * 6, transcendentals=n, bytes_accessed=4 * n * (2 * users + 3 * items)
        ),
    )(reduced, projected, start)


def update_kernel(cols_ref, live_ref, chosen_ref, rat_ref, res_ref, user_ref, item_ref, start_ref, upd_ref, part_ref):
    t = pl.program_id(0)
    width = rat_ref.shape[2]
    slots = rat_ref.shape[1]
    tiles = item_ref.shape[1] // width
    user = user_ref[...]
    pick = chosen_ref[t] > 0
    factors, starts, lives = [], [], []
    for k in range(slots):
        c = cols_ref[t, k]
        lives.append(live_ref[t, k] > 0)
        factor = item_ref[:, 0:width]
        start = start_ref[:, 0:width]
        for j in range(1, tiles):
            factor = jnp.where(c == j, item_ref[:, j * width : (j + 1) * width], factor)
            start = jnp.where(c == j, start_ref[:, j * width : (j + 1) * width], start)
        factors.append(factor)
        starts.append(start)
    estimate = lax.dot_general(
        user, jnp.concatenate(factors, axis=1), (((0,), (0,)), ((), ())), preferred_element_type=jnp.float32
    )
    fresh = []
    for k in range(slots):
        live = lives[k]
        value = jnp.where(
            live & pick,
            rat_ref[0, k].astype(jnp.float32) - estimate[:, k * width : (k + 1) * width],
            res_ref[0, k].astype(jnp.float32),
        )
        value = jnp.where(live, value, 0.0).astype(jnp.bfloat16)
        upd_ref[0, k] = value
        fresh.append(value)
    acc = lax.dot_general(
        jnp.concatenate(starts, axis=1),
        jnp.concatenate(fresh, axis=1),
        (((1,), (1,)), ((), ())),
        preferred_element_type=jnp.float32,
    )
    part_ref[...] = acc


def update(ratings, residual, tile_columns, occupied, chosen, user_factors, items, start):
    rows, slots, width, _ = ratings.shape
    rank = user_factors.shape[0]
    block = start.shape[0]
    smem = pl.BlockSpec(memory_space=pltpu.SMEM)
    tile = pl.BlockSpec((1, slots, width, width), lambda t: (t, 0, 0, 0))
    return pl.pallas_call(
        update_kernel,
        grid=(rows,),
        out_shape=(
            jax.ShapeDtypeStruct(ratings.shape, jnp.bfloat16),
            jax.ShapeDtypeStruct((block, rows * width), jnp.float32),
        ),
        in_specs=[
            smem,
            smem,
            smem,
            tile,
            tile,
            pl.BlockSpec((rank, width), lambda t: (0, t)),
            pl.BlockSpec(items.shape, lambda t: (0, 0)),
            pl.BlockSpec(start.shape, lambda t: (0, 0)),
        ],
        out_specs=(tile, pl.BlockSpec((block, width), lambda t: (0, t))),
        cost_estimate=pl.CostEstimate(
            flops=2 * rows * slots * width * width * (rank + block),
            transcendentals=0,
            bytes_accessed=6 * ratings.size + 4 * block * rows * width,
        ),
    )(tile_columns, occupied, chosen, ratings, residual, user_factors, items, start)


def local(
    ratings, residual, tile_columns, occupied, chosen, user_factors, item_factors, start_block
):
    rows_dev = ratings.shape[0]
    width = ratings.shape[2]
    block_size = start_block.shape[1]
    item_count = item_factors.shape[2] // width
    user_total = user_factors.shape[1] * lax.axis_size("users")
    updated, partial_products = update(
        ratings, residual, tile_columns, occupied, chosen, user_factors, item_factors[0], start_block[0]
    )
    projected = all_sum(partial_products, "items")
    gram_part = jnp.dot(projected, projected.T, precision=lax.Precision.HIGHEST)
    slot_terms = jnp.einsum(
        "jta,tkab->jtkb",
        projected.reshape(block_size, rows_dev, width),
        updated.astype(jnp.float32),
        precision=lax.Precision.HIGHEST,
    )
    one_hot = (
        tile_columns[:, :, None] == jnp.arange(item_count, dtype=jnp.int32)[None, None, :]
    ).astype(jnp.float32)
    item_terms = jnp.einsum("jtkb,tkc->jcb", slot_terms, one_hot, precision=lax.Precision.HIGHEST)
    item_terms = item_terms.reshape(block_size, item_count * width)
    lanes = -(-block_size // width) * width
    gram_lanes = jnp.pad(gram_part, ((0, 0), (0, lanes - block_size)))
    reduced = all_sum(jnp.concatenate([gram_lanes, item_terms], axis=1), "users")
    left_block, right_block = tail(reduced, projected, start_block[0], user_total)
    right_block = right_block.reshape(1, block_size, item_count * width)
    return (updated, left_block, right_block)


def solution(mesh):
    placed = (
        P("users", "items", None, None),
        P("users", "items", None, None),
        P("users", "items"),
        P("users", "items"),
        P("users"),
        P(None, "users"),
        P("items", None, None),
        P("items", None, None),
    )
    return jax.shard_map(
        local,
        mesh=mesh,
        in_specs=placed,
        out_specs=(P("users", "items", None, None), P(None, "users"), P("items", None, None)),
        check_vma=False,
    )
```

```python
import functools

import jax
import jax.numpy as jnp
from jax import lax
from jax.experimental import pallas as pl
from jax.experimental.pallas import tpu as pltpu
from jax.sharding import PartitionSpec as P


def all_sum(x, axis):
    n = lax.axis_size(axis)
    if n & (n - 1):
        return lax.psum(x, axis)
    step = 1
    while step < n:
        x = x + lax.ppermute(x, axis, [(i, i ^ step) for i in range(n)])
        step *= 2
    return x


def tail_kernel(reduced_ref, proj_hbm, start_hbm, left_hbm, right_ref, proj_buf, start_buf, left_buf, sems, *, scale, root):
    fetch_proj = pltpu.make_async_copy(proj_hbm, proj_buf, sems.at[0])
    fetch_start = pltpu.make_async_copy(start_hbm, start_buf, sems.at[1])
    fetch_proj.start()
    fetch_start.start()
    n = start_buf.shape[0]
    lanes = reduced_ref.shape[1] - start_buf.shape[1]
    g = reduced_ref[:, :n] * scale
    g = 0.5 * (g + g.T)
    rows = lax.broadcasted_iota(jnp.int32, (n, 2 * n), 0)
    cols = lax.broadcasted_iota(jnp.int32, (n, 2 * n), 1)
    aug = jnp.concatenate([g, (rows[:, :n] == cols[:, :n]).astype(jnp.float32)], axis=1)
    for k in range(n):
        inv_pivot = lax.rsqrt(aug[k : k + 1, k : k + 1])
        head = aug[k : k + 1, :] * inv_pivot
        factor = jnp.where(rows[:, :1] > k, aug[:, k : k + 1] * inv_pivot, 0.0)
        aug = jnp.where(rows == k, head, aug - factor * head)
    upper = aug[:, :n]
    inverse = aug[:, n:]
    hi = lax.Precision.HIGHEST
    fetch_proj.wait()
    left_buf[...] = jnp.dot(inverse, proj_buf[...], precision=hi, preferred_element_type=jnp.float32)
    store_left = pltpu.make_async_copy(left_buf, left_hbm, sems.at[2])
    store_left.start()
    summed = jnp.dot(inverse, reduced_ref[:, lanes:], precision=hi, preferred_element_type=jnp.float32)
    fetch_start.wait()
    start_term = jnp.dot(
        upper, start_buf[...].astype(jnp.float32), precision=hi, preferred_element_type=jnp.float32
    )
    right_ref[...] = summed / root - root * start_term
    store_left.wait()


def tail(reduced, projected, start, user_total):
    n, users = projected.shape
    items = start.shape[1]
    vmem = pl.BlockSpec(memory_space=pltpu.VMEM)
    anywhere = pl.BlockSpec(memory_space=pl.ANY)
    return pl.pallas_call(
        functools.partial(tail_kernel, scale=1.0 / user_total, root=float(user_total) ** 0.5),
        out_shape=(
            jax.ShapeDtypeStruct((n, users), jnp.float32),
            jax.ShapeDtypeStruct((n, items), jnp.float32),
        ),
        in_specs=[vmem, anywhere, anywhere],
        out_specs=(anywhere, vmem),
        scratch_shapes=[
            pltpu.VMEM((n, users), jnp.float32),
            pltpu.VMEM(start.shape, start.dtype),
            pltpu.VMEM((n, users), jnp.float32),
            pltpu.SemaphoreType.DMA((3,)),
        ],
        cost_estimate=pl.CostEstimate(
            flops=2 * n * n * (users + 2 * items) * 6, transcendentals=n, bytes_accessed=4 * n * (2 * users + 3 * items)
        ),
    )(reduced, projected, start)


def update_kernel(cols_ref, live_ref, chosen_ref, rat_ref, res_ref, user_ref, item_ref, start_ref, upd_ref, part_ref):
    t = pl.program_id(0)
    width = rat_ref.shape[2]
    slots = rat_ref.shape[1]
    tiles = item_ref.shape[1] // width
    user = user_ref[...]
    pick = chosen_ref[t] > 0
    factors, starts, lives = [], [], []
    for k in range(slots):
        c = cols_ref[t, k]
        lives.append(live_ref[t, k] > 0)
        factor = item_ref[:, 0:width]
        start = start_ref[:, 0:width]
        for j in range(1, tiles):
            factor = jnp.where(c == j, item_ref[:, j * width : (j + 1) * width], factor)
            start = jnp.where(c == j, start_ref[:, j * width : (j + 1) * width], start)
        factors.append(factor)
        starts.append(start)
    estimate = lax.dot_general(
        user, jnp.concatenate(factors, axis=1), (((0,), (0,)), ((), ())), preferred_element_type=jnp.float32
    )
    fresh = []
    for k in range(slots):
        live = lives[k]
        value = jnp.where(
            live & pick,
            rat_ref[0, k].astype(jnp.float32) - estimate[:, k * width : (k + 1) * width],
            res_ref[0, k].astype(jnp.float32),
        )
        value = jnp.where(live, value, 0.0).astype(jnp.bfloat16)
        upd_ref[0, k] = value
        fresh.append(value)
    acc = lax.dot_general(
        jnp.concatenate(starts, axis=1),
        jnp.concatenate(fresh, axis=1),
        (((1,), (1,)), ((), ())),
        preferred_element_type=jnp.float32,
    )
    part_ref[...] = acc


def update(ratings, residual, tile_columns, occupied, chosen, user_factors, items, start):
    rows, slots, width, _ = ratings.shape
    rank = user_factors.shape[0]
    block = start.shape[0]
    smem = pl.BlockSpec(memory_space=pltpu.SMEM)
    tile = pl.BlockSpec((1, slots, width, width), lambda t: (t, 0, 0, 0))
    return pl.pallas_call(
        update_kernel,
        grid=(rows,),
        out_shape=(
            jax.ShapeDtypeStruct(ratings.shape, jnp.bfloat16),
            jax.ShapeDtypeStruct((block, rows * width), jnp.float32),
        ),
        in_specs=[
            smem,
            smem,
            smem,
            tile,
            tile,
            pl.BlockSpec((rank, width), lambda t: (0, t)),
            pl.BlockSpec(items.shape, lambda t: (0, 0)),
            pl.BlockSpec(start.shape, lambda t: (0, 0)),
        ],
        out_specs=(tile, pl.BlockSpec((block, width), lambda t: (0, t))),
        cost_estimate=pl.CostEstimate(
            flops=2 * rows * slots * width * width * (rank + block),
            transcendentals=0,
            bytes_accessed=6 * ratings.size + 4 * block * rows * width,
        ),
    )(tile_columns, occupied, chosen, ratings, residual, user_factors, items, start)


def local(
    ratings, residual, tile_columns, occupied, chosen, user_factors, item_factors, start_block
):
    rows_dev = ratings.shape[0]
    width = ratings.shape[2]
    block_size = start_block.shape[1]
    item_count = item_factors.shape[2] // width
    user_total = user_factors.shape[1] * lax.axis_size("users")
    updated, partial_products = update(
        ratings, residual, tile_columns, occupied, chosen, user_factors, item_factors[0], start_block[0]
    )
    projected = all_sum(partial_products, "items")
    gram_part = jnp.dot(projected, projected.T, precision=lax.Precision.HIGHEST)
    slot_terms = jnp.einsum(
        "jta,tkab->jtkb",
        projected.reshape(block_size, rows_dev, width),
        updated.astype(jnp.float32),
        precision=lax.Precision.HIGHEST,
    )
    one_hot = (
        tile_columns[:, :, None] == jnp.arange(item_count, dtype=jnp.int32)[None, None, :]
    ).astype(jnp.float32)
    item_terms = jnp.einsum("jtkb,tkc->jcb", slot_terms, one_hot, precision=lax.Precision.HIGHEST)
    item_terms = item_terms.reshape(block_size, item_count * width)
    lanes = -(-block_size // width) * width
    gram_lanes = jnp.pad(gram_part, ((0, 0), (0, lanes - block_size)))
    reduced = all_sum(jnp.concatenate([gram_lanes, item_terms], axis=1), "users")
    left_block, right_block = tail(reduced, projected, start_block[0], user_total)
    right_block = right_block.reshape(1, block_size, item_count * width)
    return (updated, left_block, right_block)


def solution(mesh):
    placed = (
        P("users", "items", None, None),
        P("users", "items", None, None),
        P("users", "items"),
        P("users", "items"),
        P("users"),
        P(None, "users"),
        P("items", None, None),
        P("items", None, None),
    )
    return jax.shard_map(
        local,
        mesh=mesh,
        in_specs=placed,
        out_specs=(P("users", "items", None, None), P(None, "users"), P("items", None, None)),
        check_vma=False,
    )
```

```python
import functools

import jax
import jax.numpy as jnp
from jax import lax
from jax.experimental import pallas as pl
from jax.experimental.pallas import tpu as pltpu
from jax.sharding import PartitionSpec as P


def all_sum(x, axis):
    n = lax.axis_size(axis)
    if n & (n - 1):
        return lax.psum(x, axis)
    step = 1
    while step < n:
        x = x + lax.ppermute(x, axis, [(i, i ^ step) for i in range(n)])
        step *= 2
    return x


def split(x):
    head = x.astype(jnp.bfloat16)
    return head, (x - head.astype(jnp.float32)).astype(jnp.bfloat16)


def tail_kernel(reduced_ref, proj_ref, start_ref, left_ref, right_ref, *, scale, root):
    n = start_ref.shape[0]
    lanes = reduced_ref.shape[1] - start_ref.shape[1]
    g = reduced_ref[:, :n] * scale
    g = 0.5 * (g + g.T)
    rows = lax.broadcasted_iota(jnp.int32, (n, 2 * n), 0)
    cols = lax.broadcasted_iota(jnp.int32, (n, 2 * n), 1)
    aug = jnp.concatenate([g, (rows[:, :n] == cols[:, :n]).astype(jnp.float32)], axis=1)
    for k in range(n):
        inv_pivot = lax.rsqrt(aug[k : k + 1, k : k + 1])
        head = aug[k : k + 1, :] * inv_pivot
        factor = jnp.where(rows[:, :1] > k, aug[:, k : k + 1] * inv_pivot, 0.0)
        aug = jnp.where(rows == k, head, aug - factor * head)
    upper = aug[:, :n]
    inverse = aug[:, n:]
    f32 = jnp.float32
    inv_head, inv_tail = split(inverse)
    up_head, up_tail = split(upper)

    def product(x):
        x_head, x_tail = split(x)
        return jnp.dot(inv_head, x_head, preferred_element_type=f32) + (
            jnp.dot(inv_head, x_tail, preferred_element_type=f32) + jnp.dot(inv_tail, x_head, preferred_element_type=f32)
        )

    left_ref[...] = product(proj_ref[...])
    summed = product(reduced_ref[:, lanes:])
    start = start_ref[...]
    start_term = jnp.dot(up_head, start, preferred_element_type=f32) + jnp.dot(up_tail, start, preferred_element_type=f32)
    right_ref[...] = summed / root - root * start_term


def tail(reduced, projected, start, user_total):
    n, users = projected.shape
    items = start.shape[1]
    vmem = pl.BlockSpec(memory_space=pltpu.VMEM)
    return pl.pallas_call(
        functools.partial(tail_kernel, scale=1.0 / user_total, root=float(user_total) ** 0.5),
        out_shape=(
            jax.ShapeDtypeStruct((n, users), jnp.float32),
            jax.ShapeDtypeStruct((n, items), jnp.float32),
        ),
        in_specs=[vmem] * 3,
        out_specs=(vmem, vmem),
        cost_estimate=pl.CostEstimate(
            flops=2 * n * n * (users + 2 * items) * 3, transcendentals=n, bytes_accessed=4 * n * (2 * users + 3 * items)
        ),
    )(reduced, projected, start)


def update_kernel(cols_ref, live_ref, chosen_ref, rat_ref, res_ref, user_ref, item_ref, start_ref, upd_ref, part_ref):
    t = pl.program_id(0)
    width = rat_ref.shape[2]
    slots = rat_ref.shape[1]
    tiles = item_ref.shape[1] // width
    user = user_ref[...]
    pick = chosen_ref[t] > 0
    factors, starts, lives = [], [], []
    for k in range(slots):
        c = cols_ref[t, k]
        lives.append(live_ref[t, k] > 0)
        factor = item_ref[:, 0:width]
        start = start_ref[:, 0:width]
        for j in range(1, tiles):
            factor = jnp.where(c == j, item_ref[:, j * width : (j + 1) * width], factor)
            start = jnp.where(c == j, start_ref[:, j * width : (j + 1) * width], start)
        factors.append(factor)
        starts.append(start)
    estimate = lax.dot_general(
        user, jnp.concatenate(factors, axis=1), (((0,), (0,)), ((), ())), preferred_element_type=jnp.float32
    )
    fresh = []
    for k in range(slots):
        live = lives[k]
        value = jnp.where(
            live & pick,
            rat_ref[0, k].astype(jnp.float32) - estimate[:, k * width : (k + 1) * width],
            res_ref[0, k].astype(jnp.float32),
        )
        value = jnp.where(live, value, 0.0).astype(jnp.bfloat16)
        upd_ref[0, k] = value
        fresh.append(value)
    acc = lax.dot_general(
        jnp.concatenate(starts, axis=1),
        jnp.concatenate(fresh, axis=1),
        (((1,), (1,)), ((), ())),
        preferred_element_type=jnp.float32,
    )
    part_ref[...] = acc


def update(ratings, residual, tile_columns, occupied, chosen, user_factors, items, start):
    rows, slots, width, _ = ratings.shape
    rank = user_factors.shape[0]
    block = start.shape[0]
    smem = pl.BlockSpec(memory_space=pltpu.SMEM)
    tile = pl.BlockSpec((1, slots, width, width), lambda t: (t, 0, 0, 0))
    return pl.pallas_call(
        update_kernel,
        grid=(rows,),
        out_shape=(
            jax.ShapeDtypeStruct(ratings.shape, jnp.bfloat16),
            jax.ShapeDtypeStruct((block, rows * width), jnp.float32),
        ),
        in_specs=[
            smem,
            smem,
            smem,
            tile,
            tile,
            pl.BlockSpec((rank, width), lambda t: (0, t)),
            pl.BlockSpec(items.shape, lambda t: (0, 0)),
            pl.BlockSpec(start.shape, lambda t: (0, 0)),
        ],
        out_specs=(tile, pl.BlockSpec((block, width), lambda t: (0, t))),
        cost_estimate=pl.CostEstimate(
            flops=2 * rows * slots * width * width * (rank + block),
            transcendentals=0,
            bytes_accessed=6 * ratings.size + 4 * block * rows * width,
        ),
    )(tile_columns, occupied, chosen, ratings, residual, user_factors, items, start)


def local(
    ratings, residual, tile_columns, occupied, chosen, user_factors, item_factors, start_block
):
    rows_dev = ratings.shape[0]
    width = ratings.shape[2]
    block_size = start_block.shape[1]
    item_count = item_factors.shape[2] // width
    user_total = user_factors.shape[1] * lax.axis_size("users")
    updated, partial_products = update(
        ratings, residual, tile_columns, occupied, chosen, user_factors, item_factors[0], start_block[0]
    )
    projected = all_sum(partial_products, "items")
    gram_part = jnp.dot(projected, projected.T, precision=lax.Precision.HIGHEST)
    slot_terms = jnp.einsum(
        "jta,tkab->jtkb",
        projected.reshape(block_size, rows_dev, width),
        updated.astype(jnp.float32),
        precision=lax.Precision.HIGHEST,
    )
    one_hot = (
        tile_columns[:, :, None] == jnp.arange(item_count, dtype=jnp.int32)[None, None, :]
    ).astype(jnp.float32)
    item_terms = jnp.einsum("jtkb,tkc->jcb", slot_terms, one_hot, precision=lax.Precision.HIGHEST)
    item_terms = item_terms.reshape(block_size, item_count * width)
    lanes = -(-block_size // width) * width
    gram_lanes = jnp.pad(gram_part, ((0, 0), (0, lanes - block_size)))
    reduced = all_sum(jnp.concatenate([gram_lanes, item_terms], axis=1), "users")
    left_block, right_block = tail(reduced, projected, start_block[0], user_total)
    right_block = right_block.reshape(1, block_size, item_count * width)
    return (updated, left_block, right_block)


def solution(mesh):
    placed = (
        P("users", "items", None, None),
        P("users", "items", None, None),
        P("users", "items"),
        P("users", "items"),
        P("users"),
        P(None, "users"),
        P("items", None, None),
        P("items", None, None),
    )
    return jax.shard_map(
        local,
        mesh=mesh,
        in_specs=placed,
        out_specs=(P("users", "items", None, None), P(None, "users"), P("items", None, None)),
        check_vma=False,
    )
```

```python
import functools

import jax
import jax.numpy as jnp
from jax import lax
from jax.experimental import pallas as pl
from jax.experimental.pallas import tpu as pltpu
from jax.sharding import PartitionSpec as P


def all_sum(x, axis):
    n = lax.axis_size(axis)
    if n & (n - 1):
        return lax.psum(x, axis)
    step = 1
    while step < n:
        x = x + lax.ppermute(x, axis, [(i, i ^ step) for i in range(n)])
        step *= 2
    return x


def split(x):
    head = x.astype(jnp.bfloat16)
    return head, (x - head.astype(jnp.float32)).astype(jnp.bfloat16)


def tail_kernel(reduced_ref, proj_ref, start_ref, left_ref, right_ref, *, scale, root):
    n = start_ref.shape[0]
    lanes = reduced_ref.shape[1] - start_ref.shape[1]
    g = reduced_ref[:, :n] * scale
    g = 0.5 * (g + g.T)
    rows = lax.broadcasted_iota(jnp.int32, (n, 2 * n), 0)
    cols = lax.broadcasted_iota(jnp.int32, (n, 2 * n), 1)
    aug = jnp.concatenate([g, (rows[:, :n] == cols[:, :n]).astype(jnp.float32)], axis=1)
    for k in range(n):
        inv_pivot = lax.rsqrt(aug[k : k + 1, k : k + 1])
        head = aug[k : k + 1, :] * inv_pivot
        factor = jnp.where(rows[:, :1] > k, aug[:, k : k + 1] * inv_pivot, 0.0)
        aug = jnp.where(rows == k, head, aug - factor * head)
    upper = aug[:, :n]
    inverse = aug[:, n:]
    f32 = jnp.float32
    inv_head, inv_tail = split(inverse)
    up_head, up_tail = split(upper)

    def product(x):
        x_head, x_tail = split(x)
        return jnp.dot(inv_head, x_head, preferred_element_type=f32) + (
            jnp.dot(inv_head, x_tail, preferred_element_type=f32) + jnp.dot(inv_tail, x_head, preferred_element_type=f32)
        )

    left_ref[...] = product(proj_ref[...])
    summed = product(reduced_ref[:, lanes:])
    start = start_ref[...]
    start_term = jnp.dot(up_head, start, preferred_element_type=f32) + jnp.dot(up_tail, start, preferred_element_type=f32)
    right_ref[...] = summed / root - root * start_term


def tail(reduced, projected, start, user_total):
    n, users = projected.shape
    items = start.shape[1]
    vmem = pl.BlockSpec(memory_space=pltpu.VMEM)
    return pl.pallas_call(
        functools.partial(tail_kernel, scale=1.0 / user_total, root=float(user_total) ** 0.5),
        out_shape=(
            jax.ShapeDtypeStruct((n, users), jnp.float32),
            jax.ShapeDtypeStruct((n, items), jnp.float32),
        ),
        in_specs=[vmem] * 3,
        out_specs=(vmem, vmem),
        cost_estimate=pl.CostEstimate(
            flops=2 * n * n * (users + 2 * items) * 3, transcendentals=n, bytes_accessed=4 * n * (2 * users + 3 * items)
        ),
    )(reduced, projected, start)


def update_kernel(cols_ref, live_ref, chosen_ref, rat_ref, res_ref, user_ref, item_ref, start_ref, upd_ref, part_ref):
    group, slots, width, _ = rat_ref.shape
    tiles = item_ref.shape[1] // width
    for r in range(group):
        t = pl.program_id(0) * group + r
        user = user_ref[:, r * width : (r + 1) * width]
        pick = chosen_ref[t] > 0
        factors, starts, lives = [], [], []
        for k in range(slots):
            c = cols_ref[t, k]
            lives.append(live_ref[t, k] > 0)
            factor = item_ref[:, 0:width]
            start = start_ref[:, 0:width]
            for j in range(1, tiles):
                factor = jnp.where(c == j, item_ref[:, j * width : (j + 1) * width], factor)
                start = jnp.where(c == j, start_ref[:, j * width : (j + 1) * width], start)
            factors.append(factor)
            starts.append(start)
        estimate = lax.dot_general(
            user, jnp.concatenate(factors, axis=1), (((0,), (0,)), ((), ())), preferred_element_type=jnp.float32
        )
        fresh = []
        for k in range(slots):
            live = lives[k]
            value = jnp.where(
                live & pick,
                rat_ref[r, k].astype(jnp.float32) - estimate[:, k * width : (k + 1) * width],
                res_ref[r, k].astype(jnp.float32),
            )
            value = jnp.where(live, value, 0.0).astype(jnp.bfloat16)
            upd_ref[r, k] = value
            fresh.append(value)
        part_ref[:, r * width : (r + 1) * width] = lax.dot_general(
            jnp.concatenate(starts, axis=1),
            jnp.concatenate(fresh, axis=1),
            (((1,), (1,)), ((), ())),
            preferred_element_type=jnp.float32,
        )


def update(ratings, residual, tile_columns, occupied, chosen, user_factors, items, start):
    rows, slots, width, _ = ratings.shape
    rank = user_factors.shape[0]
    block = start.shape[0]
    group = 2 if rows % 2 == 0 else 1
    smem = pl.BlockSpec(memory_space=pltpu.SMEM)
    tile = pl.BlockSpec((group, slots, width, width), lambda t: (t, 0, 0, 0))
    return pl.pallas_call(
        update_kernel,
        grid=(rows // group,),
        out_shape=(
            jax.ShapeDtypeStruct(ratings.shape, jnp.bfloat16),
            jax.ShapeDtypeStruct((block, rows * width), jnp.float32),
        ),
        in_specs=[
            smem,
            smem,
            smem,
            tile,
            tile,
            pl.BlockSpec((rank, group * width), lambda t: (0, t)),
            pl.BlockSpec(items.shape, lambda t: (0, 0)),
            pl.BlockSpec(start.shape, lambda t: (0, 0)),
        ],
        out_specs=(tile, pl.BlockSpec((block, group * width), lambda t: (0, t))),
        cost_estimate=pl.CostEstimate(
            flops=2 * rows * slots * width * width * (rank + block),
            transcendentals=0,
            bytes_accessed=6 * ratings.size + 4 * block * rows * width,
        ),
    )(tile_columns, occupied, chosen, ratings, residual, user_factors, items, start)


def local(
    ratings, residual, tile_columns, occupied, chosen, user_factors, item_factors, start_block
):
    rows_dev = ratings.shape[0]
    width = ratings.shape[2]
    block_size = start_block.shape[1]
    item_count = item_factors.shape[2] // width
    user_total = user_factors.shape[1] * lax.axis_size("users")
    updated, partial_products = update(
        ratings, residual, tile_columns, occupied, chosen, user_factors, item_factors[0], start_block[0]
    )
    projected = all_sum(partial_products, "items")
    gram_part = jnp.dot(projected, projected.T, precision=lax.Precision.HIGHEST)
    slot_terms = jnp.einsum(
        "jta,tkab->jtkb",
        projected.reshape(block_size, rows_dev, width),
        updated.astype(jnp.float32),
        precision=lax.Precision.HIGHEST,
    )
    one_hot = (
        tile_columns[:, :, None] == jnp.arange(item_count, dtype=jnp.int32)[None, None, :]
    ).astype(jnp.float32)
    item_terms = jnp.einsum("jtkb,tkc->jcb", slot_terms, one_hot, precision=lax.Precision.HIGHEST)
    item_terms = item_terms.reshape(block_size, item_count * width)
    lanes = -(-block_size // width) * width
    gram_lanes = jnp.pad(gram_part, ((0, 0), (0, lanes - block_size)))
    reduced = all_sum(jnp.concatenate([gram_lanes, item_terms], axis=1), "users")
    left_block, right_block = tail(reduced, projected, start_block[0], user_total)
    right_block = right_block.reshape(1, block_size, item_count * width)
    return (updated, left_block, right_block)


def solution(mesh):
    placed = (
        P("users", "items", None, None),
        P("users", "items", None, None),
        P("users", "items"),
        P("users", "items"),
        P("users"),
        P(None, "users"),
        P("items", None, None),
        P("items", None, None),
    )
    return jax.shard_map(
        local,
        mesh=mesh,
        in_specs=placed,
        out_specs=(P("users", "items", None, None), P(None, "users"), P("items", None, None)),
        check_vma=False,
    )
```

```python
import functools

import jax
import jax.numpy as jnp
from jax import lax
from jax.experimental import pallas as pl
from jax.experimental.pallas import tpu as pltpu
from jax.sharding import PartitionSpec as P


def all_sum(x, axis):
    n = lax.axis_size(axis)
    if n & (n - 1):
        return lax.psum(x, axis)
    step = 1
    while step < n:
        x = x + lax.ppermute(x, axis, [(i, i ^ step) for i in range(n)])
        step *= 2
    return x


def split(x):
    head = x.astype(jnp.bfloat16)
    return head, (x - head.astype(jnp.float32)).astype(jnp.bfloat16)


def tail_kernel(reduced_ref, proj_ref, start_ref, left_ref, right_ref, *, scale, root):
    n = start_ref.shape[0]
    lanes = reduced_ref.shape[1] - start_ref.shape[1]
    g = reduced_ref[:, :n] * scale
    g = 0.5 * (g + g.T)
    rows = lax.broadcasted_iota(jnp.int32, (n, 2 * n), 0)
    cols = lax.broadcasted_iota(jnp.int32, (n, 2 * n), 1)
    aug = jnp.concatenate([g, (rows[:, :n] == cols[:, :n]).astype(jnp.float32)], axis=1)
    for k in range(n):
        inv_pivot = lax.rsqrt(aug[k : k + 1, k : k + 1])
        head = aug[k : k + 1, :] * inv_pivot
        factor = jnp.where(rows[:, :1] > k, aug[:, k : k + 1] * inv_pivot, 0.0)
        aug = jnp.where(rows == k, head, aug - factor * head)
    upper = aug[:, :n]
    inverse = aug[:, n:]
    f32 = jnp.float32
    inv_head, inv_tail = split(inverse)
    up_head, up_tail = split(upper)

    def product(x):
        x_head, x_tail = split(x)
        return jnp.dot(inv_head, x_head, preferred_element_type=f32) + (
            jnp.dot(inv_head, x_tail, preferred_element_type=f32) + jnp.dot(inv_tail, x_head, preferred_element_type=f32)
        )

    left_ref[...] = product(proj_ref[...])
    summed = product(reduced_ref[:, lanes:])
    start = start_ref[...]
    start_term = jnp.dot(up_head, start, preferred_element_type=f32) + jnp.dot(up_tail, start, preferred_element_type=f32)
    right_ref[...] = summed / root - root * start_term


def tail(reduced, projected, start, user_total):
    n, users = projected.shape
    items = start.shape[1]
    vmem = pl.BlockSpec(memory_space=pltpu.VMEM)
    return pl.pallas_call(
        functools.partial(tail_kernel, scale=1.0 / user_total, root=float(user_total) ** 0.5),
        out_shape=(
            jax.ShapeDtypeStruct((n, users), jnp.float32),
            jax.ShapeDtypeStruct((n, items), jnp.float32),
        ),
        in_specs=[vmem] * 3,
        out_specs=(vmem, vmem),
        cost_estimate=pl.CostEstimate(
            flops=2 * n * n * (users + 2 * items) * 3, transcendentals=n, bytes_accessed=4 * n * (2 * users + 3 * items)
        ),
    )(reduced, projected, start)


def update_kernel(cols_ref, live_ref, chosen_ref, rat_ref, res_ref, user_ref, item_ref, start_ref, upd_ref, part_ref):
    group, slots, width, _ = rat_ref.shape
    tiles = item_ref.shape[1] // width
    for r in range(group):
        t = pl.program_id(0) * group + r
        user = user_ref[:, r * width : (r + 1) * width]
        pick = chosen_ref[t] > 0
        factors, starts, lives = [], [], []
        for k in range(slots):
            c = cols_ref[t, k]
            lives.append(live_ref[t, k] > 0)
            factor = item_ref[:, 0:width]
            start = start_ref[:, 0:width]
            for j in range(1, tiles):
                factor = jnp.where(c == j, item_ref[:, j * width : (j + 1) * width], factor)
                start = jnp.where(c == j, start_ref[:, j * width : (j + 1) * width], start)
            factors.append(factor)
            starts.append(start)
        estimate = lax.dot_general(
            user, jnp.concatenate(factors, axis=1), (((0,), (0,)), ((), ())), preferred_element_type=jnp.float32
        )
        fresh = []
        for k in range(slots):
            live = lives[k]
            value = jnp.where(
                live & pick,
                rat_ref[r, k].astype(jnp.float32) - estimate[:, k * width : (k + 1) * width],
                res_ref[r, k].astype(jnp.float32),
            )
            value = jnp.where(live, value, 0.0).astype(jnp.bfloat16)
            upd_ref[r, k] = value
            fresh.append(value)
        part_ref[:, r * width : (r + 1) * width] = lax.dot_general(
            jnp.concatenate(starts, axis=1),
            jnp.concatenate(fresh, axis=1),
            (((1,), (1,)), ((), ())),
            preferred_element_type=jnp.float32,
        )


def update(ratings, residual, tile_columns, occupied, chosen, user_factors, items, start):
    rows, slots, width, _ = ratings.shape
    rank = user_factors.shape[0]
    block = start.shape[0]
    group = rows
    smem = pl.BlockSpec(memory_space=pltpu.SMEM)
    tile = pl.BlockSpec((group, slots, width, width), lambda t: (t, 0, 0, 0))
    return pl.pallas_call(
        update_kernel,
        grid=(rows // group,),
        out_shape=(
            jax.ShapeDtypeStruct(ratings.shape, jnp.bfloat16),
            jax.ShapeDtypeStruct((block, rows * width), jnp.float32),
        ),
        in_specs=[
            smem,
            smem,
            smem,
            tile,
            tile,
            pl.BlockSpec((rank, group * width), lambda t: (0, t)),
            pl.BlockSpec(items.shape, lambda t: (0, 0)),
            pl.BlockSpec(start.shape, lambda t: (0, 0)),
        ],
        out_specs=(tile, pl.BlockSpec((block, group * width), lambda t: (0, t))),
        cost_estimate=pl.CostEstimate(
            flops=2 * rows * slots * width * width * (rank + block),
            transcendentals=0,
            bytes_accessed=6 * ratings.size + 4 * block * rows * width,
        ),
    )(tile_columns, occupied, chosen, ratings, residual, user_factors, items, start)


def local(
    ratings, residual, tile_columns, occupied, chosen, user_factors, item_factors, start_block
):
    rows_dev = ratings.shape[0]
    width = ratings.shape[2]
    block_size = start_block.shape[1]
    item_count = item_factors.shape[2] // width
    user_total = user_factors.shape[1] * lax.axis_size("users")
    updated, partial_products = update(
        ratings, residual, tile_columns, occupied, chosen, user_factors, item_factors[0], start_block[0]
    )
    projected = all_sum(partial_products, "items")
    gram_part = jnp.dot(projected, projected.T, precision=lax.Precision.HIGHEST)
    slot_terms = jnp.einsum(
        "jta,tkab->jtkb",
        projected.reshape(block_size, rows_dev, width),
        updated.astype(jnp.float32),
        precision=lax.Precision.HIGHEST,
    )
    one_hot = (
        tile_columns[:, :, None] == jnp.arange(item_count, dtype=jnp.int32)[None, None, :]
    ).astype(jnp.float32)
    item_terms = jnp.einsum("jtkb,tkc->jcb", slot_terms, one_hot, precision=lax.Precision.HIGHEST)
    item_terms = item_terms.reshape(block_size, item_count * width)
    lanes = -(-block_size // width) * width
    gram_lanes = jnp.pad(gram_part, ((0, 0), (0, lanes - block_size)))
    reduced = all_sum(jnp.concatenate([gram_lanes, item_terms], axis=1), "users")
    left_block, right_block = tail(reduced, projected, start_block[0], user_total)
    right_block = right_block.reshape(1, block_size, item_count * width)
    return (updated, left_block, right_block)


def solution(mesh):
    placed = (
        P("users", "items", None, None),
        P("users", "items", None, None),
        P("users", "items"),
        P("users", "items"),
        P("users"),
        P(None, "users"),
        P("items", None, None),
        P("items", None, None),
    )
    return jax.shard_map(
        local,
        mesh=mesh,
        in_specs=placed,
        out_specs=(P("users", "items", None, None), P(None, "users"), P("items", None, None)),
        check_vma=False,
    )
```

```python
import functools

import jax
import jax.numpy as jnp
from jax import lax
from jax.experimental import pallas as pl
from jax.experimental.pallas import tpu as pltpu
from jax.sharding import PartitionSpec as P


def all_sum(x, axis):
    n = lax.axis_size(axis)
    if n & (n - 1):
        return lax.psum(x, axis)
    step = 1
    while step < n:
        x = x + lax.ppermute(x, axis, [(i, i ^ step) for i in range(n)])
        step *= 2
    return x


def split(x):
    head = x.astype(jnp.bfloat16)
    return head, (x - head.astype(jnp.float32)).astype(jnp.bfloat16)


def tail_kernel(reduced_ref, proj_ref, start_ref, left_ref, right_ref, *, scale, root):
    n = start_ref.shape[0]
    lanes = reduced_ref.shape[1] - start_ref.shape[1]
    g = reduced_ref[:, :n] * scale
    g = 0.5 * (g + g.T)
    rows = lax.broadcasted_iota(jnp.int32, (n, 2 * n), 0)
    cols = lax.broadcasted_iota(jnp.int32, (n, 2 * n), 1)
    aug = jnp.concatenate([g, (rows[:, :n] == cols[:, :n]).astype(jnp.float32)], axis=1)
    k = 0
    while k + 1 < n:
        p, q = k, k + 1
        inv_p = lax.rsqrt(aug[p : p + 1, p : p + 1])
        head_p = aug[p : p + 1, :] * inv_p
        factor_p = jnp.where(rows[:, :1] > p, aug[:, p : p + 1] * inv_p, 0.0)
        row_q = aug[q : q + 1, :] - factor_p[q : q + 1, :] * head_p
        inv_q = lax.rsqrt(row_q[:, q : q + 1])
        head_q = row_q * inv_q
        factor_q = jnp.where(rows[:, :1] > q, (aug[:, q : q + 1] - factor_p * head_p[:, q : q + 1]) * inv_q, 0.0)
        rest = (aug - factor_p * head_p) - factor_q * head_q
        aug = jnp.where(rows == p, head_p, jnp.where(rows == q, head_q, rest))
        k += 2
    if k < n:
        inv_pivot = lax.rsqrt(aug[k : k + 1, k : k + 1])
        head = aug[k : k + 1, :] * inv_pivot
        factor = jnp.where(rows[:, :1] > k, aug[:, k : k + 1] * inv_pivot, 0.0)
        aug = jnp.where(rows == k, head, aug - factor * head)
    upper = aug[:, :n]
    inverse = aug[:, n:]
    f32 = jnp.float32
    inv_head, inv_tail = split(inverse)
    up_head, up_tail = split(upper)

    def product(x):
        x_head, x_tail = split(x)
        return jnp.dot(inv_head, x_head, preferred_element_type=f32) + (
            jnp.dot(inv_head, x_tail, preferred_element_type=f32) + jnp.dot(inv_tail, x_head, preferred_element_type=f32)
        )

    left_ref[...] = product(proj_ref[...])
    summed = product(reduced_ref[:, lanes:])
    start = start_ref[...]
    start_term = jnp.dot(up_head, start, preferred_element_type=f32) + jnp.dot(up_tail, start, preferred_element_type=f32)
    right_ref[...] = summed / root - root * start_term


def tail(reduced, projected, start, user_total):
    n, users = projected.shape
    items = start.shape[1]
    vmem = pl.BlockSpec(memory_space=pltpu.VMEM)
    return pl.pallas_call(
        functools.partial(tail_kernel, scale=1.0 / user_total, root=float(user_total) ** 0.5),
        out_shape=(
            jax.ShapeDtypeStruct((n, users), jnp.float32),
            jax.ShapeDtypeStruct((n, items), jnp.float32),
        ),
        in_specs=[vmem] * 3,
        out_specs=(vmem, vmem),
        cost_estimate=pl.CostEstimate(
            flops=2 * n * n * (users + 2 * items) * 3, transcendentals=n, bytes_accessed=4 * n * (2 * users + 3 * items)
        ),
    )(reduced, projected, start)


def update_kernel(cols_ref, live_ref, chosen_ref, rat_ref, res_ref, user_ref, item_ref, start_ref, upd_ref, part_ref):
    group, slots, width, _ = rat_ref.shape
    tiles = item_ref.shape[1] // width
    for r in range(group):
        t = pl.program_id(0) * group + r
        user = user_ref[:, r * width : (r + 1) * width]
        pick = chosen_ref[t] > 0
        factors, starts, lives = [], [], []
        for k in range(slots):
            c = cols_ref[t, k]
            lives.append(live_ref[t, k] > 0)
            factor = item_ref[:, 0:width]
            start = start_ref[:, 0:width]
            for j in range(1, tiles):
                factor = jnp.where(c == j, item_ref[:, j * width : (j + 1) * width], factor)
                start = jnp.where(c == j, start_ref[:, j * width : (j + 1) * width], start)
            factors.append(factor)
            starts.append(start)
        estimate = lax.dot_general(
            user, jnp.concatenate(factors, axis=1), (((0,), (0,)), ((), ())), preferred_element_type=jnp.float32
        )
        fresh = []
        for k in range(slots):
            live = lives[k]
            value = jnp.where(
                live & pick,
                rat_ref[r, k].astype(jnp.float32) - estimate[:, k * width : (k + 1) * width],
                res_ref[r, k].astype(jnp.float32),
            )
            value = jnp.where(live, value, 0.0).astype(jnp.bfloat16)
            upd_ref[r, k] = value
            fresh.append(value)
        part_ref[:, r * width : (r + 1) * width] = lax.dot_general(
            jnp.concatenate(starts, axis=1),
            jnp.concatenate(fresh, axis=1),
            (((1,), (1,)), ((), ())),
            preferred_element_type=jnp.float32,
        )


def update(ratings, residual, tile_columns, occupied, chosen, user_factors, items, start):
    rows, slots, width, _ = ratings.shape
    rank = user_factors.shape[0]
    block = start.shape[0]
    group = rows
    smem = pl.BlockSpec(memory_space=pltpu.SMEM)
    tile = pl.BlockSpec((group, slots, width, width), lambda t: (t, 0, 0, 0))
    return pl.pallas_call(
        update_kernel,
        grid=(rows // group,),
        out_shape=(
            jax.ShapeDtypeStruct(ratings.shape, jnp.bfloat16),
            jax.ShapeDtypeStruct((block, rows * width), jnp.float32),
        ),
        in_specs=[
            smem,
            smem,
            smem,
            tile,
            tile,
            pl.BlockSpec((rank, group * width), lambda t: (0, t)),
            pl.BlockSpec(items.shape, lambda t: (0, 0)),
            pl.BlockSpec(start.shape, lambda t: (0, 0)),
        ],
        out_specs=(tile, pl.BlockSpec((block, group * width), lambda t: (0, t))),
        cost_estimate=pl.CostEstimate(
            flops=2 * rows * slots * width * width * (rank + block),
            transcendentals=0,
            bytes_accessed=6 * ratings.size + 4 * block * rows * width,
        ),
    )(tile_columns, occupied, chosen, ratings, residual, user_factors, items, start)


def local(
    ratings, residual, tile_columns, occupied, chosen, user_factors, item_factors, start_block
):
    rows_dev = ratings.shape[0]
    width = ratings.shape[2]
    block_size = start_block.shape[1]
    item_count = item_factors.shape[2] // width
    user_total = user_factors.shape[1] * lax.axis_size("users")
    updated, partial_products = update(
        ratings, residual, tile_columns, occupied, chosen, user_factors, item_factors[0], start_block[0]
    )
    projected = all_sum(partial_products, "items")
    gram_part = jnp.dot(projected, projected.T, precision=lax.Precision.HIGHEST)
    slot_terms = jnp.einsum(
        "jta,tkab->jtkb",
        projected.reshape(block_size, rows_dev, width),
        updated.astype(jnp.float32),
        precision=lax.Precision.HIGHEST,
    )
    one_hot = (
        tile_columns[:, :, None] == jnp.arange(item_count, dtype=jnp.int32)[None, None, :]
    ).astype(jnp.float32)
    item_terms = jnp.einsum("jtkb,tkc->jcb", slot_terms, one_hot, precision=lax.Precision.HIGHEST)
    item_terms = item_terms.reshape(block_size, item_count * width)
    lanes = -(-block_size // width) * width
    gram_lanes = jnp.pad(gram_part, ((0, 0), (0, lanes - block_size)))
    reduced = all_sum(jnp.concatenate([gram_lanes, item_terms], axis=1), "users")
    left_block, right_block = tail(reduced, projected, start_block[0], user_total)
    right_block = right_block.reshape(1, block_size, item_count * width)
    return (updated, left_block, right_block)


def solution(mesh):
    placed = (
        P("users", "items", None, None),
        P("users", "items", None, None),
        P("users", "items"),
        P("users", "items"),
        P("users"),
        P(None, "users"),
        P("items", None, None),
        P("items", None, None),
    )
    return jax.shard_map(
        local,
        mesh=mesh,
        in_specs=placed,
        out_specs=(P("users", "items", None, None), P(None, "users"), P("items", None, None)),
        check_vma=False,
    )
```

```python
import functools

import jax
import jax.numpy as jnp
from jax import lax
from jax.experimental import pallas as pl
from jax.experimental.pallas import tpu as pltpu
from jax.sharding import PartitionSpec as P


def all_sum(x, axis):
    n = lax.axis_size(axis)
    if n & (n - 1):
        return lax.psum(x, axis)
    step = 1
    while step < n:
        x = x + lax.ppermute(x, axis, [(i, i ^ step) for i in range(n)])
        step *= 2
    return x


def all_sum_parts(x, axis):
    n = lax.axis_size(axis)
    if n & (n - 1):
        return lax.psum(x, axis), jnp.zeros_like(x)
    step = 1
    other = jnp.zeros_like(x)
    while step < n:
        if step > 1:
            x = x + other
        other = lax.ppermute(x, axis, [(i, i ^ step) for i in range(n)])
        step *= 2
    return x, other


def split(x):
    head = x.astype(jnp.bfloat16)
    return head, (x - head.astype(jnp.float32)).astype(jnp.bfloat16)


def tail_kernel(reduced_ref, mine_ref, other_ref, start_ref, left_ref, right_ref, *, scale, root):
    n = start_ref.shape[0]
    lanes = reduced_ref.shape[1] - start_ref.shape[1]
    g = reduced_ref[:, :n] * scale
    g = 0.5 * (g + g.T)
    rows = lax.broadcasted_iota(jnp.int32, (n, 2 * n), 0)
    cols = lax.broadcasted_iota(jnp.int32, (n, 2 * n), 1)
    aug = jnp.concatenate([g, (rows[:, :n] == cols[:, :n]).astype(jnp.float32)], axis=1)
    for k in range(n):
        inv_pivot = lax.rsqrt(aug[k : k + 1, k : k + 1])
        head = aug[k : k + 1, :] * inv_pivot
        factor = jnp.where(rows[:, :1] > k, aug[:, k : k + 1] * inv_pivot, 0.0)
        aug = jnp.where(rows == k, head, aug - factor * head)
    upper = aug[:, :n]
    inverse = aug[:, n:]
    f32 = jnp.float32
    inv_head, inv_tail = split(inverse)
    up_head, up_tail = split(upper)

    def product(x):
        x_head, x_tail = split(x)
        return jnp.dot(inv_head, x_head, preferred_element_type=f32) + (
            jnp.dot(inv_head, x_tail, preferred_element_type=f32) + jnp.dot(inv_tail, x_head, preferred_element_type=f32)
        )

    left_ref[...] = product(mine_ref[...] + other_ref[...])
    summed = product(reduced_ref[:, lanes:])
    start = start_ref[...]
    start_term = jnp.dot(up_head, start, preferred_element_type=f32) + jnp.dot(up_tail, start, preferred_element_type=f32)
    right_ref[...] = summed / root - root * start_term


def tail(reduced, mine, other, start, user_total):
    n, users = mine.shape
    items = start.shape[1]
    vmem = pl.BlockSpec(memory_space=pltpu.VMEM)
    return pl.pallas_call(
        functools.partial(tail_kernel, scale=1.0 / user_total, root=float(user_total) ** 0.5),
        out_shape=(
            jax.ShapeDtypeStruct((n, users), jnp.float32),
            jax.ShapeDtypeStruct((n, items), jnp.float32),
        ),
        in_specs=[vmem] * 4,
        out_specs=(vmem, vmem),
        cost_estimate=pl.CostEstimate(
            flops=2 * n * n * (users + 2 * items) * 3, transcendentals=n, bytes_accessed=4 * n * (2 * users + 3 * items)
        ),
    )(reduced, mine, other, start)


def update_kernel(cols_ref, live_ref, chosen_ref, rat_ref, res_ref, user_ref, item_ref, start_ref, upd_ref, part_ref):
    group, slots, width, _ = rat_ref.shape
    tiles = item_ref.shape[1] // width
    for r in range(group):
        t = pl.program_id(0) * group + r
        user = user_ref[:, r * width : (r + 1) * width]
        pick = chosen_ref[t] > 0
        factors, starts, lives = [], [], []
        for k in range(slots):
            c = cols_ref[t, k]
            lives.append(live_ref[t, k] > 0)
            factor = item_ref[:, 0:width]
            start = start_ref[:, 0:width]
            for j in range(1, tiles):
                factor = jnp.where(c == j, item_ref[:, j * width : (j + 1) * width], factor)
                start = jnp.where(c == j, start_ref[:, j * width : (j + 1) * width], start)
            factors.append(factor)
            starts.append(start)
        estimate = lax.dot_general(
            user, jnp.concatenate(factors, axis=1), (((0,), (0,)), ((), ())), preferred_element_type=jnp.float32
        )
        fresh = []
        for k in range(slots):
            live = lives[k]
            value = jnp.where(
                live & pick,
                rat_ref[r, k].astype(jnp.float32) - estimate[:, k * width : (k + 1) * width],
                res_ref[r, k].astype(jnp.float32),
            )
            value = jnp.where(live, value, 0.0).astype(jnp.bfloat16)
            upd_ref[r, k] = value
            fresh.append(value)
        part_ref[:, r * width : (r + 1) * width] = lax.dot_general(
            jnp.concatenate(starts, axis=1),
            jnp.concatenate(fresh, axis=1),
            (((1,), (1,)), ((), ())),
            preferred_element_type=jnp.float32,
        )


def update(ratings, residual, tile_columns, occupied, chosen, user_factors, items, start):
    rows, slots, width, _ = ratings.shape
    rank = user_factors.shape[0]
    block = start.shape[0]
    group = rows
    smem = pl.BlockSpec(memory_space=pltpu.SMEM)
    tile = pl.BlockSpec((group, slots, width, width), lambda t: (t, 0, 0, 0))
    return pl.pallas_call(
        update_kernel,
        grid=(rows // group,),
        out_shape=(
            jax.ShapeDtypeStruct(ratings.shape, jnp.bfloat16),
            jax.ShapeDtypeStruct((block, rows * width), jnp.float32),
        ),
        in_specs=[
            smem,
            smem,
            smem,
            tile,
            tile,
            pl.BlockSpec((rank, group * width), lambda t: (0, t)),
            pl.BlockSpec(items.shape, lambda t: (0, 0)),
            pl.BlockSpec(start.shape, lambda t: (0, 0)),
        ],
        out_specs=(tile, pl.BlockSpec((block, group * width), lambda t: (0, t))),
        cost_estimate=pl.CostEstimate(
            flops=2 * rows * slots * width * width * (rank + block),
            transcendentals=0,
            bytes_accessed=6 * ratings.size + 4 * block * rows * width,
        ),
    )(tile_columns, occupied, chosen, ratings, residual, user_factors, items, start)


def local(
    ratings, residual, tile_columns, occupied, chosen, user_factors, item_factors, start_block
):
    rows_dev = ratings.shape[0]
    width = ratings.shape[2]
    block_size = start_block.shape[1]
    item_count = item_factors.shape[2] // width
    user_total = user_factors.shape[1] * lax.axis_size("users")
    updated, partial_products = update(
        ratings, residual, tile_columns, occupied, chosen, user_factors, item_factors[0], start_block[0]
    )
    mine, other = all_sum_parts(partial_products, "items")
    projected = mine + other
    gram_part = jnp.dot(projected, projected.T, precision=lax.Precision.HIGHEST)
    slot_terms = jnp.einsum(
        "jta,tkab->jtkb",
        projected.reshape(block_size, rows_dev, width),
        updated.astype(jnp.float32),
        precision=lax.Precision.HIGHEST,
    )
    one_hot = (
        tile_columns[:, :, None] == jnp.arange(item_count, dtype=jnp.int32)[None, None, :]
    ).astype(jnp.float32)
    item_terms = jnp.einsum("jtkb,tkc->jcb", slot_terms, one_hot, precision=lax.Precision.HIGHEST)
    item_terms = item_terms.reshape(block_size, item_count * width)
    lanes = -(-block_size // width) * width
    gram_lanes = jnp.pad(gram_part, ((0, 0), (0, lanes - block_size)))
    reduced = all_sum(jnp.concatenate([gram_lanes, item_terms], axis=1), "users")
    left_block, right_block = tail(reduced, mine, other, start_block[0], user_total)
    right_block = right_block.reshape(1, block_size, item_count * width)
    return (updated, left_block, right_block)


def solution(mesh):
    placed = (
        P("users", "items", None, None),
        P("users", "items", None, None),
        P("users", "items"),
        P("users", "items"),
        P("users"),
        P(None, "users"),
        P("items", None, None),
        P("items", None, None),
    )
    return jax.shard_map(
        local,
        mesh=mesh,
        in_specs=placed,
        out_specs=(P("users", "items", None, None), P(None, "users"), P("items", None, None)),
        check_vma=False,
    )
```

```python
import functools

import jax
import jax.numpy as jnp
from jax import lax
from jax.experimental import pallas as pl
from jax.experimental.pallas import tpu as pltpu
from jax.sharding import PartitionSpec as P


def all_sum(x, axis):
    n = lax.axis_size(axis)
    if n & (n - 1):
        return lax.psum(x, axis)
    step = 1
    while step < n:
        x = x + lax.ppermute(x, axis, [(i, i ^ step) for i in range(n)])
        step *= 2
    return x


def all_sum_parts(x, axis):
    n = lax.axis_size(axis)
    if n & (n - 1):
        return lax.psum(x, axis), jnp.zeros_like(x)
    step = 1
    other = jnp.zeros_like(x)
    while step < n:
        if step > 1:
            x = x + other
        other = lax.ppermute(x, axis, [(i, i ^ step) for i in range(n)])
        step *= 2
    return x, other


def split(x):
    head = x.astype(jnp.bfloat16)
    return head, (x - head.astype(jnp.float32)).astype(jnp.bfloat16)


def tail_kernel(reduced_ref, mine_ref, other_ref, start_ref, left_ref, right_ref, *, scale, root):
    n = start_ref.shape[0]
    lanes = reduced_ref.shape[1] - start_ref.shape[1]
    g = reduced_ref[:, :n] * scale
    g = 0.5 * (g + g.T)
    rows = lax.broadcasted_iota(jnp.int32, (n, 2 * n), 0)
    cols = lax.broadcasted_iota(jnp.int32, (n, 2 * n), 1)
    aug = jnp.concatenate([g, (rows[:, :n] == cols[:, :n]).astype(jnp.float32)], axis=1)
    for k in range(n):
        inv_pivot = lax.rsqrt(aug[k : k + 1, k : k + 1])
        head = aug[k : k + 1, :] * inv_pivot
        factor = jnp.where(rows[:, :1] > k, aug[:, k : k + 1] * inv_pivot, 0.0)
        aug = jnp.where(rows == k, head, aug - factor * head)
    upper = aug[:, :n]
    inverse = aug[:, n:]
    f32 = jnp.float32
    inv_head, inv_tail = split(inverse)
    up_head, up_tail = split(upper)

    def product(x):
        x_head, x_tail = split(x)
        return jnp.dot(inv_head, x_head, preferred_element_type=f32) + (
            jnp.dot(inv_head, x_tail, preferred_element_type=f32) + jnp.dot(inv_tail, x_head, preferred_element_type=f32)
        )

    left_ref[...] = product(mine_ref[...] + other_ref[...])
    summed = product(reduced_ref[:, lanes:])
    start = start_ref[...]
    start_term = jnp.dot(up_head, start, preferred_element_type=f32) + jnp.dot(up_tail, start, preferred_element_type=f32)
    right_ref[...] = summed / root - root * start_term


def tail(reduced, mine, other, start, user_total):
    n, users = mine.shape
    items = start.shape[1]
    vmem = pl.BlockSpec(memory_space=pltpu.VMEM)
    return pl.pallas_call(
        functools.partial(tail_kernel, scale=1.0 / user_total, root=float(user_total) ** 0.5),
        out_shape=(
            jax.ShapeDtypeStruct((n, users), jnp.float32),
            jax.ShapeDtypeStruct((n, items), jnp.float32),
        ),
        in_specs=[vmem] * 4,
        out_specs=(vmem, vmem),
        cost_estimate=pl.CostEstimate(
            flops=2 * n * n * (users + 2 * items) * 3, transcendentals=n, bytes_accessed=4 * n * (2 * users + 3 * items)
        ),
    )(reduced, mine, other, start)


def update_kernel(cols_ref, live_ref, chosen_ref, rat_ref, res_ref, user_ref, item_ref, start_ref, upd_ref, part_ref):
    group, slots, width, _ = rat_ref.shape
    tiles = item_ref.shape[1] // width
    for r in range(group):
        t = pl.program_id(0) * group + r
        user = user_ref[:, r * width : (r + 1) * width]
        pick = chosen_ref[t] > 0
        factors, starts, lives = [], [], []
        for k in range(slots):
            c = cols_ref[t, k]
            lives.append(live_ref[t, k] > 0)
            factor = item_ref[:, 0:width]
            start = start_ref[:, 0:width]
            for j in range(1, tiles):
                factor = jnp.where(c == j, item_ref[:, j * width : (j + 1) * width], factor)
                start = jnp.where(c == j, start_ref[:, j * width : (j + 1) * width], start)
            factors.append(factor)
            starts.append(start)
        estimate = lax.dot_general(
            user, jnp.concatenate(factors, axis=1), (((0,), (0,)), ((), ())), preferred_element_type=jnp.float32
        )
        fresh = []
        for k in range(slots):
            live = lives[k]
            value = jnp.where(
                live & pick,
                rat_ref[r, k].astype(jnp.float32) - estimate[:, k * width : (k + 1) * width],
                res_ref[r, k].astype(jnp.float32),
            )
            value = jnp.where(live, value, 0.0).astype(jnp.bfloat16)
            upd_ref[r, k] = value
            fresh.append(value)
        part_ref[:, r * width : (r + 1) * width] = lax.dot_general(
            jnp.concatenate(starts, axis=1),
            jnp.concatenate(fresh, axis=1),
            (((1,), (1,)), ((), ())),
            preferred_element_type=jnp.float32,
        )


def update(ratings, residual, tile_columns, occupied, chosen, user_factors, items, start):
    rows, slots, width, _ = ratings.shape
    rank = user_factors.shape[0]
    block = start.shape[0]
    group = rows
    smem = pl.BlockSpec(memory_space=pltpu.SMEM)
    tile = pl.BlockSpec((group, slots, width, width), lambda t: (t, 0, 0, 0))
    return pl.pallas_call(
        update_kernel,
        grid=(rows // group,),
        out_shape=(
            jax.ShapeDtypeStruct(ratings.shape, jnp.bfloat16),
            jax.ShapeDtypeStruct((block, rows * width), jnp.float32),
        ),
        in_specs=[
            smem,
            smem,
            smem,
            tile,
            tile,
            pl.BlockSpec((rank, group * width), lambda t: (0, t)),
            pl.BlockSpec(items.shape, lambda t: (0, 0)),
            pl.BlockSpec(start.shape, lambda t: (0, 0)),
        ],
        out_specs=(tile, pl.BlockSpec((block, group * width), lambda t: (0, t))),
        cost_estimate=pl.CostEstimate(
            flops=2 * rows * slots * width * width * (rank + block),
            transcendentals=0,
            bytes_accessed=6 * ratings.size + 4 * block * rows * width,
        ),
    )(tile_columns, occupied, chosen, ratings, residual, user_factors, items, start)


def local(
    ratings, residual, tile_columns, occupied, chosen, user_factors, item_factors, start_block
):
    rows_dev = ratings.shape[0]
    width = ratings.shape[2]
    block_size = start_block.shape[1]
    item_count = item_factors.shape[2] // width
    user_total = user_factors.shape[1] * lax.axis_size("users")
    updated, partial_products = update(
        ratings, residual, tile_columns, occupied, chosen, user_factors, item_factors[0], start_block[0]
    )
    mine, other = all_sum_parts(partial_products, "items")
    projected = mine + other
    head, low = split(projected)
    f32 = jnp.float32
    gram_part = jnp.dot(head, head.T, preferred_element_type=f32) + (
        jnp.dot(head, low.T, preferred_element_type=f32) + jnp.dot(low, head.T, preferred_element_type=f32)
    )
    rows_of = lambda x: x.reshape(block_size, rows_dev, width)
    slot_terms = jnp.einsum("jta,tkab->jtkb", rows_of(head), updated, preferred_element_type=f32) + jnp.einsum(
        "jta,tkab->jtkb", rows_of(low), updated, preferred_element_type=f32
    )
    named = tile_columns[:, :, None] == jnp.arange(item_count, dtype=jnp.int32)[None, None, :]
    item_terms = jnp.sum(jnp.where(named[None, :, :, :, None], slot_terms[:, :, :, None, :], 0.0), axis=(1, 2))
    item_terms = item_terms.reshape(block_size, item_count * width)
    lanes = -(-block_size // width) * width
    gram_lanes = jnp.pad(gram_part, ((0, 0), (0, lanes - block_size)))
    reduced = all_sum(jnp.concatenate([gram_lanes, item_terms], axis=1), "users")
    left_block, right_block = tail(reduced, mine, other, start_block[0], user_total)
    right_block = right_block.reshape(1, block_size, item_count * width)
    return (updated, left_block, right_block)


def solution(mesh):
    placed = (
        P("users", "items", None, None),
        P("users", "items", None, None),
        P("users", "items"),
        P("users", "items"),
        P("users"),
        P(None, "users"),
        P("items", None, None),
        P("items", None, None),
    )
    return jax.shard_map(
        local,
        mesh=mesh,
        in_specs=placed,
        out_specs=(P("users", "items", None, None), P(None, "users"), P("items", None, None)),
        check_vma=False,
    )
```

```python
import functools

import jax
import jax.numpy as jnp
from jax import lax
from jax.experimental import pallas as pl
from jax.experimental.pallas import tpu as pltpu
from jax.sharding import PartitionSpec as P


def all_sum(x, axis):
    n = lax.axis_size(axis)
    if n & (n - 1):
        return lax.psum(x, axis)
    step = 1
    while step < n:
        x = x + lax.ppermute(x, axis, [(i, i ^ step) for i in range(n)])
        step *= 2
    return x


def all_sum_parts(x, axis):
    n = lax.axis_size(axis)
    if n & (n - 1):
        return lax.psum(x, axis), jnp.zeros_like(x)
    step = 1
    other = jnp.zeros_like(x)
    while step < n:
        if step > 1:
            x = x + other
        other = lax.ppermute(x, axis, [(i, i ^ step) for i in range(n)])
        step *= 2
    return x, other


def split(x):
    head = x.astype(jnp.bfloat16)
    return head, (x - head.astype(jnp.float32)).astype(jnp.bfloat16)


def tail_kernel(reduced_ref, mine_ref, other_ref, start_ref, left_ref, right_ref, *, scale, root):
    n = start_ref.shape[0]
    lanes = reduced_ref.shape[1] - start_ref.shape[1]
    g = reduced_ref[:, :n] * scale
    g = 0.5 * (g + g.T)
    rows = lax.broadcasted_iota(jnp.int32, (n, 2 * n), 0)
    cols = lax.broadcasted_iota(jnp.int32, (n, 2 * n), 1)
    aug = jnp.concatenate([g, (rows[:, :n] == cols[:, :n]).astype(jnp.float32)], axis=1)
    for k in range(n):
        inv_pivot = lax.rsqrt(aug[k : k + 1, k : k + 1])
        head = aug[k : k + 1, :] * inv_pivot
        factor = jnp.where(rows[:, :1] > k, aug[:, k : k + 1] * inv_pivot, 0.0)
        aug = jnp.where(rows == k, head, aug - factor * head)
    upper = aug[:, :n]
    inverse = aug[:, n:]
    f32 = jnp.float32
    inv_head, inv_tail = split(inverse)
    up_head, up_tail = split(upper)

    def product(x):
        x_head, x_tail = split(x)
        return jnp.dot(inv_head, x_head, preferred_element_type=f32) + (
            jnp.dot(inv_head, x_tail, preferred_element_type=f32) + jnp.dot(inv_tail, x_head, preferred_element_type=f32)
        )

    left_ref[...] = product(mine_ref[...] + other_ref[...])
    summed = product(reduced_ref[:, lanes:])
    start = start_ref[...]
    start_term = jnp.dot(up_head, start, preferred_element_type=f32) + jnp.dot(up_tail, start, preferred_element_type=f32)
    right_ref[...] = summed / root - root * start_term


def tail(reduced, mine, other, start, user_total):
    n, users = mine.shape
    items = start.shape[1]
    vmem = pl.BlockSpec(memory_space=pltpu.VMEM)
    return pl.pallas_call(
        functools.partial(tail_kernel, scale=1.0 / user_total, root=float(user_total) ** 0.5),
        out_shape=(
            jax.ShapeDtypeStruct((n, users), jnp.float32),
            jax.ShapeDtypeStruct((n, items), jnp.float32),
        ),
        in_specs=[vmem] * 4,
        out_specs=(vmem, vmem),
        cost_estimate=pl.CostEstimate(
            flops=2 * n * n * (users + 2 * items) * 3, transcendentals=n, bytes_accessed=4 * n * (2 * users + 3 * items)
        ),
    )(reduced, mine, other, start)


def update_kernel(cols_ref, live_ref, chosen_ref, rat_ref, res_ref, user_ref, item_ref, start_ref, out_ref, *, emit):
    group, slots, width, _ = rat_ref.shape
    tiles = item_ref.shape[1] // width
    for r in range(group):
        t = pl.program_id(0) * group + r
        user = user_ref[:, r * width : (r + 1) * width]
        pick = chosen_ref[t] > 0
        factors, starts, lives = [], [], []
        for k in range(slots):
            c = cols_ref[t, k]
            lives.append(live_ref[t, k] > 0)
            factor = item_ref[:, 0:width]
            start = start_ref[:, 0:width]
            for j in range(1, tiles):
                factor = jnp.where(c == j, item_ref[:, j * width : (j + 1) * width], factor)
                start = jnp.where(c == j, start_ref[:, j * width : (j + 1) * width], start)
            factors.append(factor)
            starts.append(start)
        estimate = lax.dot_general(
            user, jnp.concatenate(factors, axis=1), (((0,), (0,)), ((), ())), preferred_element_type=jnp.float32
        )
        fresh = []
        for k in range(slots):
            live = lives[k]
            value = jnp.where(
                live & pick,
                rat_ref[r, k].astype(jnp.float32) - estimate[:, k * width : (k + 1) * width],
                res_ref[r, k].astype(jnp.float32),
            )
            value = jnp.where(live, value, 0.0).astype(jnp.bfloat16)
            if emit == "updated":
                out_ref[r, k] = value
            fresh.append(value)
        if emit == "updated":
            continue
        out_ref[:, r * width : (r + 1) * width] = lax.dot_general(
            jnp.concatenate(starts, axis=1),
            jnp.concatenate(fresh, axis=1),
            (((1,), (1,)), ((), ())),
            preferred_element_type=jnp.float32,
        )


def update(ratings, residual, tile_columns, occupied, chosen, user_factors, items, start, emit):
    rows, slots, width, _ = ratings.shape
    rank = user_factors.shape[0]
    block = start.shape[0]
    group = rows
    smem = pl.BlockSpec(memory_space=pltpu.SMEM)
    tile = pl.BlockSpec((group, slots, width, width), lambda t: (t, 0, 0, 0))
    if emit == "updated":
        out_shape = jax.ShapeDtypeStruct(ratings.shape, jnp.bfloat16)
        out_spec = tile
    else:
        out_shape = jax.ShapeDtypeStruct((block, rows * width), jnp.float32)
        out_spec = pl.BlockSpec((block, group * width), lambda t: (0, t))
    return pl.pallas_call(
        functools.partial(update_kernel, emit=emit),
        grid=(rows // group,),
        out_shape=out_shape,
        in_specs=[
            smem,
            smem,
            smem,
            tile,
            tile,
            pl.BlockSpec((rank, group * width), lambda t: (0, t)),
            pl.BlockSpec(items.shape, lambda t: (0, 0)),
            pl.BlockSpec(start.shape, lambda t: (0, 0)),
        ],
        out_specs=out_spec,
        cost_estimate=pl.CostEstimate(
            flops=2 * rows * slots * width * width * (rank + block),
            transcendentals=0,
            bytes_accessed=6 * ratings.size + 4 * block * rows * width,
        ),
    )(tile_columns, occupied, chosen, ratings, residual, user_factors, items, start)


def local(
    ratings, residual, tile_columns, occupied, chosen, user_factors, item_factors, start_block
):
    rows_dev = ratings.shape[0]
    width = ratings.shape[2]
    block_size = start_block.shape[1]
    item_count = item_factors.shape[2] // width
    user_total = user_factors.shape[1] * lax.axis_size("users")
    inputs = (ratings, residual, tile_columns, occupied, chosen, user_factors, item_factors[0], start_block[0])
    partial_products = update(*inputs, emit="products")
    updated = update(*inputs, emit="updated")
    mine, other = all_sum_parts(partial_products, "items")
    projected = mine + other
    gram_part = jnp.dot(projected, projected.T, precision=lax.Precision.HIGHEST)
    slot_terms = jnp.einsum(
        "jta,tkab->jtkb",
        projected.reshape(block_size, rows_dev, width),
        updated.astype(jnp.float32),
        precision=lax.Precision.HIGHEST,
    )
    one_hot = (
        tile_columns[:, :, None] == jnp.arange(item_count, dtype=jnp.int32)[None, None, :]
    ).astype(jnp.float32)
    item_terms = jnp.einsum("jtkb,tkc->jcb", slot_terms, one_hot, precision=lax.Precision.HIGHEST)
    item_terms = item_terms.reshape(block_size, item_count * width)
    lanes = -(-block_size // width) * width
    gram_lanes = jnp.pad(gram_part, ((0, 0), (0, lanes - block_size)))
    reduced = all_sum(jnp.concatenate([gram_lanes, item_terms], axis=1), "users")
    left_block, right_block = tail(reduced, mine, other, start_block[0], user_total)
    right_block = right_block.reshape(1, block_size, item_count * width)
    return (updated, left_block, right_block)


def solution(mesh):
    placed = (
        P("users", "items", None, None),
        P("users", "items", None, None),
        P("users", "items"),
        P("users", "items"),
        P("users"),
        P(None, "users"),
        P("items", None, None),
        P("items", None, None),
    )
    return jax.shard_map(
        local,
        mesh=mesh,
        in_specs=placed,
        out_specs=(P("users", "items", None, None), P(None, "users"), P("items", None, None)),
        check_vma=False,
    )
```

```python
import functools

import jax
import jax.numpy as jnp
from jax import lax
from jax.experimental import pallas as pl
from jax.experimental.pallas import tpu as pltpu
from jax.sharding import PartitionSpec as P


def all_sum(x, axis):
    n = lax.axis_size(axis)
    if n & (n - 1):
        return lax.psum(x, axis)
    step = 1
    while step < n:
        x = x + lax.ppermute(x, axis, [(i, i ^ step) for i in range(n)])
        step *= 2
    return x


def all_sum_parts(x, axis):
    n = lax.axis_size(axis)
    if n & (n - 1):
        return lax.psum(x, axis), jnp.zeros_like(x)
    step = 1
    other = jnp.zeros_like(x)
    while step < n:
        if step > 1:
            x = x + other
        other = lax.ppermute(x, axis, [(i, i ^ step) for i in range(n)])
        step *= 2
    return x, other


def all_sum_split(first, second, axis):
    n = lax.axis_size(axis)
    x = jnp.concatenate([first, second], axis=1)
    cut = first.shape[1]
    if n & (n - 1) or n < 2:
        x = lax.psum(x, axis)
        return x[:, :cut], jnp.zeros_like(first), x[:, cut:], jnp.zeros_like(second)
    step = 1
    while step < n // 2:
        x = x + lax.ppermute(x, axis, [(i, i ^ step) for i in range(n)])
        step *= 2
    pairs = [(i, i ^ step) for i in range(n)]
    head, rest = x[:, :cut], x[:, cut:]
    return head, lax.ppermute(head, axis, pairs), rest, lax.ppermute(rest, axis, pairs)


def split(x):
    head = x.astype(jnp.bfloat16)
    return head, (x - head.astype(jnp.float32)).astype(jnp.bfloat16)


def factor_kernel(mine_ref, other_ref, upper_ref, inverse_ref, *, scale):
    n = upper_ref.shape[0]
    g = (mine_ref[...] + other_ref[...])[:, :n] * scale
    g = 0.5 * (g + g.T)
    rows = lax.broadcasted_iota(jnp.int32, (n, 2 * n), 0)
    cols = lax.broadcasted_iota(jnp.int32, (n, 2 * n), 1)
    aug = jnp.concatenate([g, (rows[:, :n] == cols[:, :n]).astype(jnp.float32)], axis=1)
    for k in range(n):
        inv_pivot = lax.rsqrt(aug[k : k + 1, k : k + 1])
        head = aug[k : k + 1, :] * inv_pivot
        factor = jnp.where(rows[:, :1] > k, aug[:, k : k + 1] * inv_pivot, 0.0)
        aug = jnp.where(rows == k, head, aug - factor * head)
    upper_ref[...] = aug[:, :n]
    inverse_ref[...] = aug[:, n:]


def finish_kernel(upper_ref, inverse_ref, sums_ref, last_ref, mine_ref, other_ref, start_ref, left_ref, right_ref, *, root):
    f32 = jnp.float32
    inv_head, inv_tail = split(inverse_ref[...])
    up_head, up_tail = split(upper_ref[...])

    def product(x):
        x_head, x_tail = split(x)
        return jnp.dot(inv_head, x_head, preferred_element_type=f32) + (
            jnp.dot(inv_head, x_tail, preferred_element_type=f32) + jnp.dot(inv_tail, x_head, preferred_element_type=f32)
        )

    left_ref[...] = product(mine_ref[...] + other_ref[...])
    summed = product(sums_ref[...] + last_ref[...])
    start = start_ref[...]
    start_term = jnp.dot(up_head, start, preferred_element_type=f32) + jnp.dot(up_tail, start, preferred_element_type=f32)
    right_ref[...] = summed / root - root * start_term


def tail(gram_mine, gram_other, sums, last, mine, other, start, user_total):
    n, users = mine.shape
    items = start.shape[1]
    vmem = pl.BlockSpec(memory_space=pltpu.VMEM)
    square = jax.ShapeDtypeStruct((n, n), jnp.float32)
    upper, inverse = pl.pallas_call(
        functools.partial(factor_kernel, scale=1.0 / user_total),
        out_shape=(square, square),
        in_specs=[vmem] * 2,
        out_specs=(vmem, vmem),
        cost_estimate=pl.CostEstimate(flops=4 * n * n * n, transcendentals=n, bytes_accessed=4 * n * (2 * gram_mine.shape[1] + 2 * n)),
    )(gram_mine, gram_other)
    return pl.pallas_call(
        functools.partial(finish_kernel, root=float(user_total) ** 0.5),
        out_shape=(
            jax.ShapeDtypeStruct((n, users), jnp.float32),
            jax.ShapeDtypeStruct((n, items), jnp.float32),
        ),
        in_specs=[vmem] * 7,
        out_specs=(vmem, vmem),
        cost_estimate=pl.CostEstimate(
            flops=2 * n * n * (users + 2 * items) * 3, transcendentals=0, bytes_accessed=4 * n * (2 * users + 4 * items)
        ),
    )(upper, inverse, sums, last, mine, other, start)


def update_kernel(cols_ref, live_ref, chosen_ref, rat_ref, res_ref, user_ref, item_ref, start_ref, out_ref, *, emit):
    group, slots, width, _ = rat_ref.shape
    tiles = item_ref.shape[1] // width
    for r in range(group):
        t = pl.program_id(0) * group + r
        user = user_ref[:, r * width : (r + 1) * width]
        pick = chosen_ref[t] > 0
        factors, starts, lives = [], [], []
        for k in range(slots):
            c = cols_ref[t, k]
            lives.append(live_ref[t, k] > 0)
            factor = item_ref[:, 0:width]
            start = start_ref[:, 0:width]
            for j in range(1, tiles):
                factor = jnp.where(c == j, item_ref[:, j * width : (j + 1) * width], factor)
                start = jnp.where(c == j, start_ref[:, j * width : (j + 1) * width], start)
            factors.append(factor)
            starts.append(start)
        estimate = lax.dot_general(
            user, jnp.concatenate(factors, axis=1), (((0,), (0,)), ((), ())), preferred_element_type=jnp.float32
        )
        fresh = []
        for k in range(slots):
            live = lives[k]
            value = jnp.where(
                live & pick,
                rat_ref[r, k].astype(jnp.float32) - estimate[:, k * width : (k + 1) * width],
                res_ref[r, k].astype(jnp.float32),
            )
            value = jnp.where(live, value, 0.0).astype(jnp.bfloat16)
            if emit == "updated":
                out_ref[r, k] = value
            fresh.append(value)
        if emit == "updated":
            continue
        out_ref[:, r * width : (r + 1) * width] = lax.dot_general(
            jnp.concatenate(starts, axis=1),
            jnp.concatenate(fresh, axis=1),
            (((1,), (1,)), ((), ())),
            preferred_element_type=jnp.float32,
        )


def update(ratings, residual, tile_columns, occupied, chosen, user_factors, items, start, emit):
    rows, slots, width, _ = ratings.shape
    rank = user_factors.shape[0]
    block = start.shape[0]
    group = rows
    smem = pl.BlockSpec(memory_space=pltpu.SMEM)
    tile = pl.BlockSpec((group, slots, width, width), lambda t: (t, 0, 0, 0))
    if emit == "updated":
        out_shape = jax.ShapeDtypeStruct(ratings.shape, jnp.bfloat16)
        out_spec = tile
    else:
        out_shape = jax.ShapeDtypeStruct((block, rows * width), jnp.float32)
        out_spec = pl.BlockSpec((block, group * width), lambda t: (0, t))
    return pl.pallas_call(
        functools.partial(update_kernel, emit=emit),
        grid=(rows // group,),
        out_shape=out_shape,
        in_specs=[
            smem,
            smem,
            smem,
            tile,
            tile,
            pl.BlockSpec((rank, group * width), lambda t: (0, t)),
            pl.BlockSpec(items.shape, lambda t: (0, 0)),
            pl.BlockSpec(start.shape, lambda t: (0, 0)),
        ],
        out_specs=out_spec,
        cost_estimate=pl.CostEstimate(
            flops=2 * rows * slots * width * width * (rank + block),
            transcendentals=0,
            bytes_accessed=6 * ratings.size + 4 * block * rows * width,
        ),
    )(tile_columns, occupied, chosen, ratings, residual, user_factors, items, start)


def local(
    ratings, residual, tile_columns, occupied, chosen, user_factors, item_factors, start_block
):
    rows_dev = ratings.shape[0]
    width = ratings.shape[2]
    block_size = start_block.shape[1]
    item_count = item_factors.shape[2] // width
    user_total = user_factors.shape[1] * lax.axis_size("users")
    inputs = (ratings, residual, tile_columns, occupied, chosen, user_factors, item_factors[0], start_block[0])
    partial_products = update(*inputs, emit="products")
    updated = update(*inputs, emit="updated")
    mine, other = all_sum_parts(partial_products, "items")
    projected = mine + other
    gram_part = jnp.dot(projected, projected.T, precision=lax.Precision.HIGHEST)
    slot_terms = jnp.einsum(
        "jta,tkab->jtkb",
        projected.reshape(block_size, rows_dev, width),
        updated.astype(jnp.float32),
        precision=lax.Precision.HIGHEST,
    )
    one_hot = (
        tile_columns[:, :, None] == jnp.arange(item_count, dtype=jnp.int32)[None, None, :]
    ).astype(jnp.float32)
    item_terms = jnp.einsum("jtkb,tkc->jcb", slot_terms, one_hot, precision=lax.Precision.HIGHEST)
    item_terms = item_terms.reshape(block_size, item_count * width)
    lanes = -(-block_size // width) * width
    gram_lanes = jnp.pad(gram_part, ((0, 0), (0, lanes - block_size)))
    gram_mine, gram_other, sums, last = all_sum_split(gram_lanes, item_terms, "users")
    left_block, right_block = tail(gram_mine, gram_other, sums, last, mine, other, start_block[0], user_total)
    right_block = right_block.reshape(1, block_size, item_count * width)
    return (updated, left_block, right_block)


def solution(mesh):
    placed = (
        P("users", "items", None, None),
        P("users", "items", None, None),
        P("users", "items"),
        P("users", "items"),
        P("users"),
        P(None, "users"),
        P("items", None, None),
        P("items", None, None),
    )
    return jax.shard_map(
        local,
        mesh=mesh,
        in_specs=placed,
        out_specs=(P("users", "items", None, None), P(None, "users"), P("items", None, None)),
        check_vma=False,
    )
```

```python
import functools

import jax
import jax.numpy as jnp
from jax import lax
from jax.experimental import pallas as pl
from jax.experimental.pallas import tpu as pltpu
from jax.sharding import PartitionSpec as P


def all_sum(x, axis):
    n = lax.axis_size(axis)
    if n & (n - 1):
        return lax.psum(x, axis)
    step = 1
    while step < n:
        x = x + lax.ppermute(x, axis, [(i, i ^ step) for i in range(n)])
        step *= 2
    return x


def all_sum_parts(x, axis):
    n = lax.axis_size(axis)
    if n & (n - 1):
        return lax.psum(x, axis), jnp.zeros_like(x)
    step = 1
    other = jnp.zeros_like(x)
    while step < n:
        if step > 1:
            x = x + other
        other = lax.ppermute(x, axis, [(i, i ^ step) for i in range(n)])
        step *= 2
    return x, other


def split(x):
    head = x.astype(jnp.bfloat16)
    return head, (x - head.astype(jnp.float32)).astype(jnp.bfloat16)


def tail_kernel(reduced_ref, mine_ref, other_ref, start_ref, left_ref, right_ref, *, scale, root):
    n = start_ref.shape[0]
    lanes = reduced_ref.shape[1] - start_ref.shape[1]
    g = reduced_ref[:, :n] * scale
    g = 0.5 * (g + g.T)
    rows = lax.broadcasted_iota(jnp.int32, (n, 2 * n), 0)
    cols = lax.broadcasted_iota(jnp.int32, (n, 2 * n), 1)
    aug = jnp.concatenate([g, (rows[:, :n] == cols[:, :n]).astype(jnp.float32)], axis=1)
    for k in range(n):
        inv_pivot = lax.rsqrt(aug[k : k + 1, k : k + 1])
        head = aug[k : k + 1, :] * inv_pivot
        factor = jnp.where(rows[:, :1] > k, aug[:, k : k + 1] * inv_pivot, 0.0)
        aug = jnp.where(rows == k, head, aug - factor * head)
    upper = aug[:, :n]
    inverse = aug[:, n:]
    f32 = jnp.float32
    inv_head, inv_tail = split(inverse)
    up_head, up_tail = split(upper)

    def product(x):
        x_head, x_tail = split(x)
        return jnp.dot(inv_head, x_head, preferred_element_type=f32) + (
            jnp.dot(inv_head, x_tail, preferred_element_type=f32) + jnp.dot(inv_tail, x_head, preferred_element_type=f32)
        )

    left_ref[...] = product(mine_ref[...] + other_ref[...])
    summed = product(reduced_ref[:, lanes:])
    start = start_ref[...]
    start_term = jnp.dot(up_head, start, preferred_element_type=f32) + jnp.dot(up_tail, start, preferred_element_type=f32)
    right_ref[...] = summed / root - root * start_term


def tail(reduced, mine, other, start, user_total):
    n, users = mine.shape
    items = start.shape[1]
    vmem = pl.BlockSpec(memory_space=pltpu.VMEM)
    return pl.pallas_call(
        functools.partial(tail_kernel, scale=1.0 / user_total, root=float(user_total) ** 0.5),
        out_shape=(
            jax.ShapeDtypeStruct((n, users), jnp.float32),
            jax.ShapeDtypeStruct((n, items), jnp.float32),
        ),
        in_specs=[vmem] * 4,
        out_specs=(vmem, vmem),
        cost_estimate=pl.CostEstimate(
            flops=2 * n * n * (users + 2 * items) * 3, transcendentals=n, bytes_accessed=4 * n * (2 * users + 3 * items)
        ),
    )(reduced, mine, other, start)


def update_kernel(cols_ref, live_ref, chosen_ref, rat_ref, res_ref, user_ref, item_ref, start_ref, out_ref, *, emit):
    group, slots, width, _ = rat_ref.shape
    tiles = item_ref.shape[1] // width
    for r in range(group):
        t = pl.program_id(0) * group + r
        user = user_ref[:, r * width : (r + 1) * width]
        pick = chosen_ref[t] > 0
        factors, starts, lives = [], [], []
        for k in range(slots):
            c = cols_ref[t, k]
            lives.append(live_ref[t, k] > 0)
            factor = item_ref[:, 0:width]
            start = start_ref[:, 0:width]
            for j in range(1, tiles):
                factor = jnp.where(c == j, item_ref[:, j * width : (j + 1) * width], factor)
                start = jnp.where(c == j, start_ref[:, j * width : (j + 1) * width], start)
            factors.append(factor)
            starts.append(start)
        estimate = lax.dot_general(
            user, jnp.concatenate(factors, axis=1), (((0,), (0,)), ((), ())), preferred_element_type=jnp.float32
        )
        fresh = []
        for k in range(slots):
            live = lives[k]
            value = jnp.where(
                live & pick,
                rat_ref[r, k].astype(jnp.float32) - estimate[:, k * width : (k + 1) * width],
                res_ref[r, k].astype(jnp.float32),
            )
            value = jnp.where(live, value, 0.0).astype(jnp.bfloat16)
            if emit == "updated":
                out_ref[r, k] = value
            fresh.append(value)
        if emit == "updated":
            continue
        out_ref[:, r * width : (r + 1) * width] = lax.dot_general(
            jnp.concatenate(starts, axis=1),
            jnp.concatenate(fresh, axis=1),
            (((1,), (1,)), ((), ())),
            preferred_element_type=jnp.float32,
        )


def update(ratings, residual, tile_columns, occupied, chosen, user_factors, items, start, emit):
    rows, slots, width, _ = ratings.shape
    rank = user_factors.shape[0]
    block = start.shape[0]
    group = rows
    smem = pl.BlockSpec(memory_space=pltpu.SMEM)
    tile = pl.BlockSpec((group, slots, width, width), lambda t: (t, 0, 0, 0))
    if emit == "updated":
        out_shape = jax.ShapeDtypeStruct(ratings.shape, jnp.bfloat16)
        out_spec = tile
    else:
        out_shape = jax.ShapeDtypeStruct((block, rows * width), jnp.float32)
        out_spec = pl.BlockSpec((block, group * width), lambda t: (0, t))
    return pl.pallas_call(
        functools.partial(update_kernel, emit=emit),
        grid=(rows // group,),
        out_shape=out_shape,
        in_specs=[
            smem,
            smem,
            smem,
            tile,
            tile,
            pl.BlockSpec((rank, group * width), lambda t: (0, t)),
            pl.BlockSpec(items.shape, lambda t: (0, 0)),
            pl.BlockSpec(start.shape, lambda t: (0, 0)),
        ],
        out_specs=out_spec,
        cost_estimate=pl.CostEstimate(
            flops=2 * rows * slots * width * width * (rank + block),
            transcendentals=0,
            bytes_accessed=6 * ratings.size + 4 * block * rows * width,
        ),
    )(tile_columns, occupied, chosen, ratings, residual, user_factors, items, start)


def local(
    ratings, residual, tile_columns, occupied, chosen, user_factors, item_factors, start_block
):
    rows_dev = ratings.shape[0]
    width = ratings.shape[2]
    block_size = start_block.shape[1]
    item_count = item_factors.shape[2] // width
    user_total = user_factors.shape[1] * lax.axis_size("users")
    inputs = (ratings, residual, tile_columns, occupied, chosen, user_factors, item_factors[0], start_block[0])
    partial_products = update(*inputs, emit="products")
    updated = update(*inputs, emit="updated")
    mine, other = all_sum_parts(partial_products, "items")
    projected = mine + other
    head_f32 = lax.reduce_precision(projected, exponent_bits=8, mantissa_bits=7)
    head = head_f32.astype(jnp.bfloat16)
    low = (projected - head_f32).astype(jnp.bfloat16)
    f32 = jnp.float32
    gram_part = jnp.dot(head, head.T, preferred_element_type=f32) + (
        jnp.dot(head, low.T, preferred_element_type=f32) + jnp.dot(low, head.T, preferred_element_type=f32)
    )
    rows_of = lambda x: x.reshape(block_size, rows_dev, width)
    slot_terms = jnp.einsum("jta,tkab->jtkb", rows_of(head), updated, preferred_element_type=f32) + jnp.einsum(
        "jta,tkab->jtkb", rows_of(low), updated, preferred_element_type=f32
    )
    named = tile_columns[:, :, None] == jnp.arange(item_count, dtype=jnp.int32)[None, None, :]
    item_terms = jnp.sum(jnp.where(named[None, :, :, :, None], slot_terms[:, :, :, None, :], 0.0), axis=(1, 2))
    item_terms = item_terms.reshape(block_size, item_count * width)
    lanes = -(-block_size // width) * width
    gram_lanes = jnp.pad(gram_part, ((0, 0), (0, lanes - block_size)))
    reduced = all_sum(jnp.concatenate([gram_lanes, item_terms], axis=1), "users")
    left_block, right_block = tail(reduced, mine, other, start_block[0], user_total)
    right_block = right_block.reshape(1, block_size, item_count * width)
    return (updated, left_block, right_block)


def solution(mesh):
    placed = (
        P("users", "items", None, None),
        P("users", "items", None, None),
        P("users", "items"),
        P("users", "items"),
        P("users"),
        P(None, "users"),
        P("items", None, None),
        P("items", None, None),
    )
    return jax.shard_map(
        local,
        mesh=mesh,
        in_specs=placed,
        out_specs=(P("users", "items", None, None), P(None, "users"), P("items", None, None)),
        check_vma=False,
    )
```

```python
import functools

import jax
import jax.numpy as jnp
from jax import lax
from jax.experimental import pallas as pl
from jax.experimental.pallas import tpu as pltpu
from jax.sharding import PartitionSpec as P


def all_sum(x, axis):
    n = lax.axis_size(axis)
    if n & (n - 1):
        return lax.psum(x, axis)
    step = 1
    while step < n:
        x = x + lax.ppermute(x, axis, [(i, i ^ step) for i in range(n)])
        step *= 2
    return x


def all_sum_parts(x, axis):
    n = lax.axis_size(axis)
    if n & (n - 1):
        return lax.psum(x, axis), jnp.zeros_like(x)
    step = 1
    other = jnp.zeros_like(x)
    while step < n:
        if step > 1:
            x = x + other
        other = lax.ppermute(x, axis, [(i, i ^ step) for i in range(n)])
        step *= 2
    return x, other


def split(x):
    head = x.astype(jnp.bfloat16)
    return head, (x - head.astype(jnp.float32)).astype(jnp.bfloat16)


def tail_kernel(reduced_ref, mine_ref, other_ref, start_ref, left_ref, right_ref, *, scale, root):
    n = start_ref.shape[0]
    lanes = reduced_ref.shape[1] - start_ref.shape[1]
    g = reduced_ref[:, :n] * scale
    rows = lax.broadcasted_iota(jnp.int32, (n, 2 * n), 0)
    cols = lax.broadcasted_iota(jnp.int32, (n, 2 * n), 1)
    aug = jnp.concatenate([g, (rows[:, :n] == cols[:, :n]).astype(jnp.float32)], axis=1)
    for k in range(n):
        inv_pivot = lax.rsqrt(aug[k : k + 1, k : k + 1])
        head = aug[k : k + 1, :] * inv_pivot
        factor = jnp.where(rows[:, :1] > k, aug[:, k : k + 1] * inv_pivot, 0.0)
        aug = jnp.where(rows == k, head, aug - factor * head)
    upper = aug[:, :n]
    inverse = aug[:, n:]
    f32 = jnp.float32
    inv_head, inv_tail = split(inverse)
    up_head, up_tail = split(upper)

    def product(x):
        x_head, x_tail = split(x)
        return jnp.dot(inv_head, x_head, preferred_element_type=f32) + (
            jnp.dot(inv_head, x_tail, preferred_element_type=f32) + jnp.dot(inv_tail, x_head, preferred_element_type=f32)
        )

    left_ref[...] = product(mine_ref[...] + other_ref[...])
    summed = product(reduced_ref[:, lanes:])
    start = start_ref[...]
    start_term = jnp.dot(up_head, start, preferred_element_type=f32) + jnp.dot(up_tail, start, preferred_element_type=f32)
    right_ref[...] = summed / root - root * start_term


def tail(reduced, mine, other, start, user_total):
    n, users = mine.shape
    items = start.shape[1]
    vmem = pl.BlockSpec(memory_space=pltpu.VMEM)
    return pl.pallas_call(
        functools.partial(tail_kernel, scale=1.0 / user_total, root=float(user_total) ** 0.5),
        out_shape=(
            jax.ShapeDtypeStruct((n, users), jnp.float32),
            jax.ShapeDtypeStruct((n, items), jnp.float32),
        ),
        in_specs=[vmem] * 4,
        out_specs=(vmem, vmem),
        cost_estimate=pl.CostEstimate(
            flops=2 * n * n * (users + 2 * items) * 3, transcendentals=n, bytes_accessed=4 * n * (2 * users + 3 * items)
        ),
    )(reduced, mine, other, start)


def update_kernel(cols_ref, live_ref, chosen_ref, rat_ref, res_ref, user_ref, item_ref, start_ref, out_ref, *, emit):
    group, slots, width, _ = rat_ref.shape
    tiles = item_ref.shape[1] // width
    for r in range(group):
        t = pl.program_id(0) * group + r
        user = user_ref[:, r * width : (r + 1) * width]
        pick = chosen_ref[t] > 0
        factors, starts, lives = [], [], []
        for k in range(slots):
            c = cols_ref[t, k]
            lives.append(live_ref[t, k] > 0)
            factor = item_ref[:, 0:width]
            start = start_ref[:, 0:width]
            for j in range(1, tiles):
                factor = jnp.where(c == j, item_ref[:, j * width : (j + 1) * width], factor)
                start = jnp.where(c == j, start_ref[:, j * width : (j + 1) * width], start)
            factors.append(factor)
            starts.append(start)
        estimate = lax.dot_general(
            user, jnp.concatenate(factors, axis=1), (((0,), (0,)), ((), ())), preferred_element_type=jnp.float32
        )
        fresh = []
        for k in range(slots):
            live = lives[k]
            value = jnp.where(
                live & pick,
                rat_ref[r, k].astype(jnp.float32) - estimate[:, k * width : (k + 1) * width],
                res_ref[r, k].astype(jnp.float32),
            )
            value = jnp.where(live, value, 0.0).astype(jnp.bfloat16)
            if emit == "updated":
                out_ref[r, k] = value
            fresh.append(value)
        if emit == "updated":
            continue
        out_ref[:, r * width : (r + 1) * width] = lax.dot_general(
            jnp.concatenate(starts, axis=1),
            jnp.concatenate(fresh, axis=1),
            (((1,), (1,)), ((), ())),
            preferred_element_type=jnp.float32,
        )


def update(ratings, residual, tile_columns, occupied, chosen, user_factors, items, start, emit):
    rows, slots, width, _ = ratings.shape
    rank = user_factors.shape[0]
    block = start.shape[0]
    group = rows
    smem = pl.BlockSpec(memory_space=pltpu.SMEM)
    tile = pl.BlockSpec((group, slots, width, width), lambda t: (t, 0, 0, 0))
    if emit == "updated":
        out_shape = jax.ShapeDtypeStruct(ratings.shape, jnp.bfloat16)
        out_spec = tile
    else:
        out_shape = jax.ShapeDtypeStruct((block, rows * width), jnp.float32)
        out_spec = pl.BlockSpec((block, group * width), lambda t: (0, t))
    return pl.pallas_call(
        functools.partial(update_kernel, emit=emit),
        grid=(rows // group,),
        out_shape=out_shape,
        in_specs=[
            smem,
            smem,
            smem,
            tile,
            tile,
            pl.BlockSpec((rank, group * width), lambda t: (0, t)),
            pl.BlockSpec(items.shape, lambda t: (0, 0)),
            pl.BlockSpec(start.shape, lambda t: (0, 0)),
        ],
        out_specs=out_spec,
        cost_estimate=pl.CostEstimate(
            flops=2 * rows * slots * width * width * (rank + block),
            transcendentals=0,
            bytes_accessed=6 * ratings.size + 4 * block * rows * width,
        ),
    )(tile_columns, occupied, chosen, ratings, residual, user_factors, items, start)


def local(
    ratings, residual, tile_columns, occupied, chosen, user_factors, item_factors, start_block
):
    rows_dev = ratings.shape[0]
    width = ratings.shape[2]
    block_size = start_block.shape[1]
    item_count = item_factors.shape[2] // width
    user_total = user_factors.shape[1] * lax.axis_size("users")
    inputs = (ratings, residual, tile_columns, occupied, chosen, user_factors, item_factors[0], start_block[0])
    partial_products = update(*inputs, emit="products")
    updated = update(*inputs, emit="updated")
    mine, other = all_sum_parts(partial_products, "items")
    projected = mine + other
    head_f32 = lax.reduce_precision(projected, exponent_bits=8, mantissa_bits=7)
    head = head_f32.astype(jnp.bfloat16)
    low = (projected - head_f32).astype(jnp.bfloat16)
    f32 = jnp.float32
    gram_part = jnp.dot(head, head.T, preferred_element_type=f32) + (
        jnp.dot(head, low.T, preferred_element_type=f32) + jnp.dot(low, head.T, preferred_element_type=f32)
    )
    rows_of = lambda x: x.reshape(block_size, rows_dev, width)
    slot_terms = jnp.einsum("jta,tkab->jtkb", rows_of(head), updated, preferred_element_type=f32) + jnp.einsum(
        "jta,tkab->jtkb", rows_of(low), updated, preferred_element_type=f32
    )
    named = tile_columns[:, :, None] == jnp.arange(item_count, dtype=jnp.int32)[None, None, :]
    item_terms = jnp.sum(jnp.where(named[None, :, :, :, None], slot_terms[:, :, :, None, :], 0.0), axis=(1, 2))
    item_terms = item_terms.reshape(block_size, item_count * width)
    lanes = -(-block_size // width) * width
    gram_lanes = jnp.pad(gram_part, ((0, 0), (0, lanes - block_size)))
    reduced = all_sum(jnp.concatenate([gram_lanes, item_terms], axis=1), "users")
    left_block, right_block = tail(reduced, mine, other, start_block[0], user_total)
    right_block = right_block.reshape(1, block_size, item_count * width)
    return (updated, left_block, right_block)


def solution(mesh):
    placed = (
        P("users", "items", None, None),
        P("users", "items", None, None),
        P("users", "items"),
        P("users", "items"),
        P("users"),
        P(None, "users"),
        P("items", None, None),
        P("items", None, None),
    )
    return jax.shard_map(
        local,
        mesh=mesh,
        in_specs=placed,
        out_specs=(P("users", "items", None, None), P(None, "users"), P("items", None, None)),
        check_vma=False,
    )
```

```python
import functools

import jax
import jax.numpy as jnp
from jax import lax
from jax.experimental import pallas as pl
from jax.experimental.pallas import tpu as pltpu
from jax.sharding import PartitionSpec as P


def all_sum(x, axis):
    n = lax.axis_size(axis)
    if n & (n - 1):
        return lax.psum(x, axis)
    step = n // 2
    while step >= 1:
        x = x + lax.ppermute(x, axis, [(i, i ^ step) for i in range(n)])
        step //= 2
    return x


def all_sum_parts(x, axis):
    n = lax.axis_size(axis)
    if n & (n - 1):
        return lax.psum(x, axis), jnp.zeros_like(x)
    step = 1
    other = jnp.zeros_like(x)
    while step < n:
        if step > 1:
            x = x + other
        other = lax.ppermute(x, axis, [(i, i ^ step) for i in range(n)])
        step *= 2
    return x, other


def split(x):
    head = x.astype(jnp.bfloat16)
    return head, (x - head.astype(jnp.float32)).astype(jnp.bfloat16)


def tail_kernel(reduced_ref, mine_ref, other_ref, start_ref, left_ref, right_ref, *, scale, root):
    n = start_ref.shape[0]
    lanes = reduced_ref.shape[1] - start_ref.shape[1]
    g = reduced_ref[:, :n] * scale
    g = 0.5 * (g + g.T)
    rows = lax.broadcasted_iota(jnp.int32, (n, 2 * n), 0)
    cols = lax.broadcasted_iota(jnp.int32, (n, 2 * n), 1)
    aug = jnp.concatenate([g, (rows[:, :n] == cols[:, :n]).astype(jnp.float32)], axis=1)
    for k in range(n):
        inv_pivot = lax.rsqrt(aug[k : k + 1, k : k + 1])
        head = aug[k : k + 1, :] * inv_pivot
        factor = jnp.where(rows[:, :1] > k, aug[:, k : k + 1] * inv_pivot, 0.0)
        aug = jnp.where(rows == k, head, aug - factor * head)
    upper = aug[:, :n]
    inverse = aug[:, n:]
    f32 = jnp.float32
    inv_head, inv_tail = split(inverse)
    up_head, up_tail = split(upper)

    def product(x):
        x_head, x_tail = split(x)
        return jnp.dot(inv_head, x_head, preferred_element_type=f32) + (
            jnp.dot(inv_head, x_tail, preferred_element_type=f32) + jnp.dot(inv_tail, x_head, preferred_element_type=f32)
        )

    left_ref[...] = product(mine_ref[...] + other_ref[...])
    summed = product(reduced_ref[:, lanes:])
    start = start_ref[...]
    start_term = jnp.dot(up_head, start, preferred_element_type=f32) + jnp.dot(up_tail, start, preferred_element_type=f32)
    right_ref[...] = summed / root - root * start_term


def tail(reduced, mine, other, start, user_total):
    n, users = mine.shape
    items = start.shape[1]
    vmem = pl.BlockSpec(memory_space=pltpu.VMEM)
    return pl.pallas_call(
        functools.partial(tail_kernel, scale=1.0 / user_total, root=float(user_total) ** 0.5),
        out_shape=(
            jax.ShapeDtypeStruct((n, users), jnp.float32),
            jax.ShapeDtypeStruct((n, items), jnp.float32),
        ),
        in_specs=[vmem] * 4,
        out_specs=(vmem, vmem),
        cost_estimate=pl.CostEstimate(
            flops=2 * n * n * (users + 2 * items) * 3, transcendentals=n, bytes_accessed=4 * n * (2 * users + 3 * items)
        ),
    )(reduced, mine, other, start)


def update_kernel(cols_ref, live_ref, chosen_ref, rat_ref, res_ref, user_ref, item_ref, start_ref, out_ref, *, emit):
    group, slots, width, _ = rat_ref.shape
    tiles = item_ref.shape[1] // width
    for r in range(group):
        t = pl.program_id(0) * group + r
        user = user_ref[:, r * width : (r + 1) * width]
        pick = chosen_ref[t] > 0
        factors, starts, lives = [], [], []
        for k in range(slots):
            c = cols_ref[t, k]
            lives.append(live_ref[t, k] > 0)
            factor = item_ref[:, 0:width]
            start = start_ref[:, 0:width]
            for j in range(1, tiles):
                factor = jnp.where(c == j, item_ref[:, j * width : (j + 1) * width], factor)
                start = jnp.where(c == j, start_ref[:, j * width : (j + 1) * width], start)
            factors.append(factor)
            starts.append(start)
        estimate = lax.dot_general(
            user, jnp.concatenate(factors, axis=1), (((0,), (0,)), ((), ())), preferred_element_type=jnp.float32
        )
        fresh = []
        for k in range(slots):
            live = lives[k]
            value = jnp.where(
                live & pick,
                rat_ref[r, k].astype(jnp.float32) - estimate[:, k * width : (k + 1) * width],
                res_ref[r, k].astype(jnp.float32),
            )
            value = jnp.where(live, value, 0.0).astype(jnp.bfloat16)
            if emit == "updated":
                out_ref[r, k] = value
            fresh.append(value)
        if emit == "updated":
            continue
        out_ref[:, r * width : (r + 1) * width] = lax.dot_general(
            jnp.concatenate(starts, axis=1),
            jnp.concatenate(fresh, axis=1),
            (((1,), (1,)), ((), ())),
            preferred_element_type=jnp.float32,
        )


def update(ratings, residual, tile_columns, occupied, chosen, user_factors, items, start, emit):
    rows, slots, width, _ = ratings.shape
    rank = user_factors.shape[0]
    block = start.shape[0]
    group = rows
    smem = pl.BlockSpec(memory_space=pltpu.SMEM)
    tile = pl.BlockSpec((group, slots, width, width), lambda t: (t, 0, 0, 0))
    if emit == "updated":
        out_shape = jax.ShapeDtypeStruct(ratings.shape, jnp.bfloat16)
        out_spec = tile
    else:
        out_shape = jax.ShapeDtypeStruct((block, rows * width), jnp.float32)
        out_spec = pl.BlockSpec((block, group * width), lambda t: (0, t))
    return pl.pallas_call(
        functools.partial(update_kernel, emit=emit),
        grid=(rows // group,),
        out_shape=out_shape,
        in_specs=[
            smem,
            smem,
            smem,
            tile,
            tile,
            pl.BlockSpec((rank, group * width), lambda t: (0, t)),
            pl.BlockSpec(items.shape, lambda t: (0, 0)),
            pl.BlockSpec(start.shape, lambda t: (0, 0)),
        ],
        out_specs=out_spec,
        cost_estimate=pl.CostEstimate(
            flops=2 * rows * slots * width * width * (rank + block),
            transcendentals=0,
            bytes_accessed=6 * ratings.size + 4 * block * rows * width,
        ),
    )(tile_columns, occupied, chosen, ratings, residual, user_factors, items, start)


def local(
    ratings, residual, tile_columns, occupied, chosen, user_factors, item_factors, start_block
):
    rows_dev = ratings.shape[0]
    width = ratings.shape[2]
    block_size = start_block.shape[1]
    item_count = item_factors.shape[2] // width
    user_total = user_factors.shape[1] * lax.axis_size("users")
    inputs = (ratings, residual, tile_columns, occupied, chosen, user_factors, item_factors[0], start_block[0])
    partial_products = update(*inputs, emit="products")
    updated = update(*inputs, emit="updated")
    mine, other = all_sum_parts(partial_products, "items")
    projected = mine + other
    head_f32 = lax.reduce_precision(projected, exponent_bits=8, mantissa_bits=7)
    head = head_f32.astype(jnp.bfloat16)
    low = (projected - head_f32).astype(jnp.bfloat16)
    f32 = jnp.float32
    gram_part = jnp.dot(head, head.T, preferred_element_type=f32) + (
        jnp.dot(head, low.T, preferred_element_type=f32) + jnp.dot(low, head.T, preferred_element_type=f32)
    )
    rows_of = lambda x: x.reshape(block_size, rows_dev, width)
    slot_terms = jnp.einsum("jta,tkab->jtkb", rows_of(head), updated, preferred_element_type=f32) + jnp.einsum(
        "jta,tkab->jtkb", rows_of(low), updated, preferred_element_type=f32
    )
    named = tile_columns[:, :, None] == jnp.arange(item_count, dtype=jnp.int32)[None, None, :]
    item_terms = jnp.sum(jnp.where(named[None, :, :, :, None], slot_terms[:, :, :, None, :], 0.0), axis=(1, 2))
    item_terms = item_terms.reshape(block_size, item_count * width)
    lanes = -(-block_size // width) * width
    gram_lanes = jnp.pad(gram_part, ((0, 0), (0, lanes - block_size)))
    reduced = all_sum(jnp.concatenate([gram_lanes, item_terms], axis=1), "users")
    left_block, right_block = tail(reduced, mine, other, start_block[0], user_total)
    right_block = right_block.reshape(1, block_size, item_count * width)
    return (updated, left_block, right_block)


def solution(mesh):
    placed = (
        P("users", "items", None, None),
        P("users", "items", None, None),
        P("users", "items"),
        P("users", "items"),
        P("users"),
        P(None, "users"),
        P("items", None, None),
        P("items", None, None),
    )
    return jax.shard_map(
        local,
        mesh=mesh,
        in_specs=placed,
        out_specs=(P("users", "items", None, None), P(None, "users"), P("items", None, None)),
        check_vma=False,
    )
```

```python
import functools

import jax
import jax.numpy as jnp
from jax import lax
from jax.experimental import pallas as pl
from jax.experimental.pallas import tpu as pltpu
from jax.sharding import PartitionSpec as P


def all_sum(x, axis):
    n = lax.axis_size(axis)
    if n & (n - 1):
        return lax.psum(x, axis)
    step = 1
    while step < n:
        x = x + lax.ppermute(x, axis, [(i, i ^ step) for i in range(n)])
        step *= 2
    return x


def all_sum_parts(x, axis):
    n = lax.axis_size(axis)
    if n & (n - 1):
        return lax.psum(x, axis), jnp.zeros_like(x)
    step = 1
    other = jnp.zeros_like(x)
    while step < n:
        if step > 1:
            x = x + other
        other = lax.ppermute(x, axis, [(i, i ^ step) for i in range(n)])
        step *= 2
    return x, other


def split(x):
    head = x.astype(jnp.bfloat16)
    return head, (x - head.astype(jnp.float32)).astype(jnp.bfloat16)


def tail_kernel(reduced_ref, mine_ref, other_ref, start_ref, left_ref, right_ref, *, scale, root):
    n = start_ref.shape[0]
    lanes = reduced_ref.shape[1] - start_ref.shape[1]
    g = reduced_ref[:, :n] * scale
    g = 0.5 * (g + g.T)
    rows = lax.broadcasted_iota(jnp.int32, (n, 2 * n), 0)
    cols = lax.broadcasted_iota(jnp.int32, (n, 2 * n), 1)
    aug = jnp.concatenate([g, (rows[:, :n] == cols[:, :n]).astype(jnp.float32)], axis=1)
    for k in range(n):
        inv_pivot = lax.rsqrt(aug[k : k + 1, k : k + 1])
        head = aug[k : k + 1, :] * inv_pivot
        factor = jnp.where(rows[:, :1] > k, aug[:, k : k + 1] * inv_pivot, 0.0)
        aug = jnp.where(rows == k, head, aug - factor * head)
    upper = aug[:, :n]
    inverse = aug[:, n:]
    f32 = jnp.float32
    inv_head, inv_tail = split(inverse)
    up_head, up_tail = split(upper)

    def product(x):
        x_head, x_tail = split(x)
        return jnp.dot(inv_head, x_head, preferred_element_type=f32) + (
            jnp.dot(inv_head, x_tail, preferred_element_type=f32) + jnp.dot(inv_tail, x_head, preferred_element_type=f32)
        )

    left_ref[...] = product(mine_ref[...] + other_ref[...])
    summed = product(reduced_ref[:, lanes:])
    start = start_ref[...]
    start_term = jnp.dot(up_head, start, preferred_element_type=f32) + jnp.dot(up_tail, start, preferred_element_type=f32)
    right_ref[...] = summed / root - root * start_term


def tail(reduced, mine, other, start, user_total):
    n, users = mine.shape
    items = start.shape[1]
    vmem = pl.BlockSpec(memory_space=pltpu.VMEM)
    return pl.pallas_call(
        functools.partial(tail_kernel, scale=1.0 / user_total, root=float(user_total) ** 0.5),
        out_shape=(
            jax.ShapeDtypeStruct((n, users), jnp.float32),
            jax.ShapeDtypeStruct((n, items), jnp.float32),
        ),
        in_specs=[vmem] * 4,
        out_specs=(vmem, vmem),
        cost_estimate=pl.CostEstimate(
            flops=2 * n * n * (users + 2 * items) * 3, transcendentals=n, bytes_accessed=4 * n * (2 * users + 3 * items)
        ),
    )(reduced, mine, other, start)


def update_kernel(cols_ref, live_ref, chosen_ref, rat_ref, res_ref, user_ref, item_ref, start_ref, out_ref, *, emit):
    group, slots, width, _ = rat_ref.shape
    tiles = item_ref.shape[1] // width
    for r in range(group):
        t = pl.program_id(0) * group + r
        user = user_ref[:, r * width : (r + 1) * width]
        pick = chosen_ref[t] > 0
        factors, starts, lives = [], [], []
        for k in range(slots):
            c = cols_ref[t, k]
            lives.append(live_ref[t, k] > 0)
            factor = item_ref[:, 0:width]
            start = start_ref[:, 0:width]
            for j in range(1, tiles):
                factor = jnp.where(c == j, item_ref[:, j * width : (j + 1) * width], factor)
                start = jnp.where(c == j, start_ref[:, j * width : (j + 1) * width], start)
            factors.append(factor)
            starts.append(start)
        estimate = lax.dot_general(
            user, jnp.concatenate(factors, axis=1), (((0,), (0,)), ((), ())), preferred_element_type=jnp.float32
        )
        fresh = []
        for k in range(slots):
            live = lives[k]
            value = jnp.where(
                live & pick,
                rat_ref[r, k].astype(jnp.float32) - estimate[:, k * width : (k + 1) * width],
                res_ref[r, k].astype(jnp.float32),
            )
            value = jnp.where(live, value, 0.0).astype(jnp.bfloat16)
            if emit == "updated":
                out_ref[r, k] = value
            fresh.append(value)
        if emit == "updated":
            continue
        out_ref[:, r * width : (r + 1) * width] = lax.dot_general(
            jnp.concatenate(starts, axis=1),
            jnp.concatenate(fresh, axis=1),
            (((1,), (1,)), ((), ())),
            preferred_element_type=jnp.float32,
        )


def update(ratings, residual, tile_columns, occupied, chosen, user_factors, items, start, emit):
    rows, slots, width, _ = ratings.shape
    rank = user_factors.shape[0]
    block = start.shape[0]
    group = rows // 2 if emit == "products" and rows % 2 == 0 else rows
    smem = pl.BlockSpec(memory_space=pltpu.SMEM)
    tile = pl.BlockSpec((group, slots, width, width), lambda t: (t, 0, 0, 0))
    if emit == "updated":
        out_shape = jax.ShapeDtypeStruct(ratings.shape, jnp.bfloat16)
        out_spec = tile
    else:
        out_shape = jax.ShapeDtypeStruct((block, rows * width), jnp.float32)
        out_spec = pl.BlockSpec((block, group * width), lambda t: (0, t))
    return pl.pallas_call(
        functools.partial(update_kernel, emit=emit),
        grid=(rows // group,),
        out_shape=out_shape,
        in_specs=[
            smem,
            smem,
            smem,
            tile,
            tile,
            pl.BlockSpec((rank, group * width), lambda t: (0, t)),
            pl.BlockSpec(items.shape, lambda t: (0, 0)),
            pl.BlockSpec(start.shape, lambda t: (0, 0)),
        ],
        out_specs=out_spec,
        cost_estimate=pl.CostEstimate(
            flops=2 * rows * slots * width * width * (rank + block),
            transcendentals=0,
            bytes_accessed=6 * ratings.size + 4 * block * rows * width,
        ),
    )(tile_columns, occupied, chosen, ratings, residual, user_factors, items, start)


def local(
    ratings, residual, tile_columns, occupied, chosen, user_factors, item_factors, start_block
):
    rows_dev = ratings.shape[0]
    width = ratings.shape[2]
    block_size = start_block.shape[1]
    item_count = item_factors.shape[2] // width
    user_total = user_factors.shape[1] * lax.axis_size("users")
    inputs = (ratings, residual, tile_columns, occupied, chosen, user_factors, item_factors[0], start_block[0])
    partial_products = update(*inputs, emit="products")
    updated = update(*inputs, emit="updated")
    mine, other = all_sum_parts(partial_products, "items")
    projected = mine + other
    head_f32 = lax.reduce_precision(projected, exponent_bits=8, mantissa_bits=7)
    head = head_f32.astype(jnp.bfloat16)
    low = (projected - head_f32).astype(jnp.bfloat16)
    f32 = jnp.float32
    gram_part = jnp.dot(head, head.T, preferred_element_type=f32) + (
        jnp.dot(head, low.T, preferred_element_type=f32) + jnp.dot(low, head.T, preferred_element_type=f32)
    )
    rows_of = lambda x: x.reshape(block_size, rows_dev, width)
    slot_terms = jnp.einsum("jta,tkab->jtkb", rows_of(head), updated, preferred_element_type=f32) + jnp.einsum(
        "jta,tkab->jtkb", rows_of(low), updated, preferred_element_type=f32
    )
    named = tile_columns[:, :, None] == jnp.arange(item_count, dtype=jnp.int32)[None, None, :]
    item_terms = jnp.sum(jnp.where(named[None, :, :, :, None], slot_terms[:, :, :, None, :], 0.0), axis=(1, 2))
    item_terms = item_terms.reshape(block_size, item_count * width)
    lanes = -(-block_size // width) * width
    gram_lanes = jnp.pad(gram_part, ((0, 0), (0, lanes - block_size)))
    reduced = all_sum(jnp.concatenate([gram_lanes, item_terms], axis=1), "users")
    left_block, right_block = tail(reduced, mine, other, start_block[0], user_total)
    right_block = right_block.reshape(1, block_size, item_count * width)
    return (updated, left_block, right_block)


def solution(mesh):
    placed = (
        P("users", "items", None, None),
        P("users", "items", None, None),
        P("users", "items"),
        P("users", "items"),
        P("users"),
        P(None, "users"),
        P("items", None, None),
        P("items", None, None),
    )
    return jax.shard_map(
        local,
        mesh=mesh,
        in_specs=placed,
        out_specs=(P("users", "items", None, None), P(None, "users"), P("items", None, None)),
        check_vma=False,
    )
```

```python
import functools

import jax
import jax.numpy as jnp
from jax import lax
from jax.experimental import pallas as pl
from jax.experimental.pallas import tpu as pltpu
from jax.sharding import PartitionSpec as P


def all_sum(x, axis):
    n = lax.axis_size(axis)
    if n & (n - 1):
        return lax.psum(x, axis)
    step = 1
    while step < n:
        x = x + lax.ppermute(x, axis, [(i, i ^ step) for i in range(n)])
        step *= 2
    return x


def all_sum_parts(x, axis):
    n = lax.axis_size(axis)
    if n & (n - 1):
        return lax.psum(x, axis), jnp.zeros_like(x)
    step = 1
    other = jnp.zeros_like(x)
    while step < n:
        if step > 1:
            x = x + other
        other = lax.ppermute(x, axis, [(i, i ^ step) for i in range(n)])
        step *= 2
    return x, other


def split(x):
    head = x.astype(jnp.bfloat16)
    return head, (x - head.astype(jnp.float32)).astype(jnp.bfloat16)


def tail_kernel(reduced_ref, mine_ref, other_ref, start_ref, left_ref, right_ref, *, scale, root):
    n = start_ref.shape[0]
    lanes = reduced_ref.shape[1] - start_ref.shape[1]
    g = reduced_ref[:, :n] * scale
    g = 0.5 * (g + g.T)
    rows = lax.broadcasted_iota(jnp.int32, (n, 2 * n), 0)
    cols = lax.broadcasted_iota(jnp.int32, (n, 2 * n), 1)
    aug = jnp.concatenate([g, (rows[:, :n] == cols[:, :n]).astype(jnp.float32)], axis=1)
    for k in range(n):
        inv_pivot = lax.rsqrt(aug[k : k + 1, k : k + 1])
        head = aug[k : k + 1, :] * inv_pivot
        factor = jnp.where(rows[:, :1] > k, aug[:, k : k + 1] * inv_pivot, 0.0)
        aug = jnp.where(rows == k, head, aug - factor * head)
    upper = aug[:, :n]
    inverse = aug[:, n:]
    f32 = jnp.float32
    inv_head, inv_tail = split(inverse)
    up_head, up_tail = split(upper)

    def product(x):
        x_head, x_tail = split(x)
        return jnp.dot(inv_head, x_head, preferred_element_type=f32) + (
            jnp.dot(inv_head, x_tail, preferred_element_type=f32) + jnp.dot(inv_tail, x_head, preferred_element_type=f32)
        )

    left_ref[...] = product(mine_ref[...] + other_ref[...])
    summed = product(reduced_ref[:, lanes:])
    start = start_ref[...]
    start_term = jnp.dot(up_head, start, preferred_element_type=f32) + jnp.dot(up_tail, start, preferred_element_type=f32)
    right_ref[...] = summed / root - root * start_term


def tail(reduced, mine, other, start, user_total):
    n, users = mine.shape
    items = start.shape[1]
    vmem = pl.BlockSpec(memory_space=pltpu.VMEM)
    return pl.pallas_call(
        functools.partial(tail_kernel, scale=1.0 / user_total, root=float(user_total) ** 0.5),
        out_shape=(
            jax.ShapeDtypeStruct((n, users), jnp.float32),
            jax.ShapeDtypeStruct((n, items), jnp.float32),
        ),
        in_specs=[vmem] * 4,
        out_specs=(vmem, vmem),
        cost_estimate=pl.CostEstimate(
            flops=2 * n * n * (users + 2 * items) * 3, transcendentals=n, bytes_accessed=4 * n * (2 * users + 3 * items)
        ),
    )(reduced, mine, other, start)


def update_kernel(cols_ref, live_ref, chosen_ref, rat_ref, res_ref, user_ref, item_ref, start_ref, out_ref, *, emit):
    group, slots, width, _ = rat_ref.shape
    tiles = item_ref.shape[1] // width
    for r in range(group):
        t = pl.program_id(0) * group + r
        user = user_ref[:, r * width : (r + 1) * width]
        pick = chosen_ref[t] > 0
        factors, starts, lives = [], [], []
        for k in range(slots):
            c = cols_ref[t, k]
            lives.append(live_ref[t, k] > 0)
            factor = item_ref[:, 0:width]
            start = start_ref[:, 0:width]
            for j in range(1, tiles):
                factor = jnp.where(c == j, item_ref[:, j * width : (j + 1) * width], factor)
                start = jnp.where(c == j, start_ref[:, j * width : (j + 1) * width], start)
            factors.append(factor)
            starts.append(start)
        estimate = lax.dot_general(
            user, jnp.concatenate(factors, axis=1), (((0,), (0,)), ((), ())), preferred_element_type=jnp.float32
        )
        fresh = []
        for k in range(slots):
            live = lives[k]
            value = jnp.where(
                live & pick,
                rat_ref[r, k].astype(jnp.float32) - estimate[:, k * width : (k + 1) * width],
                res_ref[r, k].astype(jnp.float32),
            )
            value = jnp.where(live, value, 0.0).astype(jnp.bfloat16)
            if emit == "updated":
                out_ref[r, k] = value
            fresh.append(value)
        if emit == "updated":
            continue
        out_ref[:, r * width : (r + 1) * width] = lax.dot_general(
            jnp.concatenate(fresh, axis=1),
            jnp.concatenate(starts, axis=1),
            (((1,), (1,)), ((), ())),
            preferred_element_type=jnp.float32,
        ).T


def update(ratings, residual, tile_columns, occupied, chosen, user_factors, items, start, emit):
    rows, slots, width, _ = ratings.shape
    rank = user_factors.shape[0]
    block = start.shape[0]
    group = rows
    smem = pl.BlockSpec(memory_space=pltpu.SMEM)
    tile = pl.BlockSpec((group, slots, width, width), lambda t: (t, 0, 0, 0))
    if emit == "updated":
        out_shape = jax.ShapeDtypeStruct(ratings.shape, jnp.bfloat16)
        out_spec = tile
    else:
        out_shape = jax.ShapeDtypeStruct((block, rows * width), jnp.float32)
        out_spec = pl.BlockSpec((block, group * width), lambda t: (0, t))
    return pl.pallas_call(
        functools.partial(update_kernel, emit=emit),
        grid=(rows // group,),
        out_shape=out_shape,
        in_specs=[
            smem,
            smem,
            smem,
            tile,
            tile,
            pl.BlockSpec((rank, group * width), lambda t: (0, t)),
            pl.BlockSpec(items.shape, lambda t: (0, 0)),
            pl.BlockSpec(start.shape, lambda t: (0, 0)),
        ],
        out_specs=out_spec,
        cost_estimate=pl.CostEstimate(
            flops=2 * rows * slots * width * width * (rank + block),
            transcendentals=0,
            bytes_accessed=6 * ratings.size + 4 * block * rows * width,
        ),
    )(tile_columns, occupied, chosen, ratings, residual, user_factors, items, start)


def local(
    ratings, residual, tile_columns, occupied, chosen, user_factors, item_factors, start_block
):
    rows_dev = ratings.shape[0]
    width = ratings.shape[2]
    block_size = start_block.shape[1]
    item_count = item_factors.shape[2] // width
    user_total = user_factors.shape[1] * lax.axis_size("users")
    inputs = (ratings, residual, tile_columns, occupied, chosen, user_factors, item_factors[0], start_block[0])
    partial_products = update(*inputs, emit="products")
    updated = update(*inputs, emit="updated")
    mine, other = all_sum_parts(partial_products, "items")
    projected = mine + other
    head_f32 = lax.reduce_precision(projected, exponent_bits=8, mantissa_bits=7)
    head = head_f32.astype(jnp.bfloat16)
    low = (projected - head_f32).astype(jnp.bfloat16)
    f32 = jnp.float32
    gram_part = jnp.dot(head, head.T, preferred_element_type=f32) + (
        jnp.dot(head, low.T, preferred_element_type=f32) + jnp.dot(low, head.T, preferred_element_type=f32)
    )
    rows_of = lambda x: x.reshape(block_size, rows_dev, width)
    slot_terms = jnp.einsum("jta,tkab->jtkb", rows_of(head), updated, preferred_element_type=f32) + jnp.einsum(
        "jta,tkab->jtkb", rows_of(low), updated, preferred_element_type=f32
    )
    named = tile_columns[:, :, None] == jnp.arange(item_count, dtype=jnp.int32)[None, None, :]
    item_terms = jnp.sum(jnp.where(named[None, :, :, :, None], slot_terms[:, :, :, None, :], 0.0), axis=(1, 2))
    item_terms = item_terms.reshape(block_size, item_count * width)
    lanes = -(-block_size // width) * width
    gram_lanes = jnp.pad(gram_part, ((0, 0), (0, lanes - block_size)))
    reduced = all_sum(jnp.concatenate([gram_lanes, item_terms], axis=1), "users")
    left_block, right_block = tail(reduced, mine, other, start_block[0], user_total)
    right_block = right_block.reshape(1, block_size, item_count * width)
    return (updated, left_block, right_block)


def solution(mesh):
    placed = (
        P("users", "items", None, None),
        P("users", "items", None, None),
        P("users", "items"),
        P("users", "items"),
        P("users"),
        P(None, "users"),
        P("items", None, None),
        P("items", None, None),
    )
    return jax.shard_map(
        local,
        mesh=mesh,
        in_specs=placed,
        out_specs=(P("users", "items", None, None), P(None, "users"), P("items", None, None)),
        check_vma=False,
    )
```
